128 devices in a mesh: dp: 4 (over z), ep: 32 (over y, x, core).
Axes of the slice: x: 4, y: 4, z: 4, core: 2. Of those that a mesh axis runs over, the one named last changes fastest.
Arguments:
- queries: bfloat16 [2048, 2, 8192], P(('dp', 'ep')), may hold values from -150 to 150
- keys_new: bfloat16 [2048, 2, 512], P(('dp', 'ep')), may hold values from -5 to 5
- values_new: bfloat16 [2048, 2, 512], P(('dp', 'ep')), may hold values from -5 to 5
- importance: float32 [2048, 2, 4], P(('dp', 'ep')), may hold values from 0.25 to 4
- merge_flags: int32 [2048, 2, 4], P(('dp', 'ep')), may hold values 0 or 1
- key_cache: bfloat16 [2048, 512, 512], P(('dp', 'ep')), may hold values from -5.1 to 5.1
- value_cache: bfloat16 [2048, 512, 512], P(('dp', 'ep')), may hold values from -5 to 5
- last_weight: float32 [2048, 4], P(('dp', 'ep')), may hold values from 0.5 to 8
- lengths: int32 [2048], P(('dp', 'ep')), may hold values from 2 to 510, as said below
- residual: bfloat16 [2048, 2, 2048], P(('dp', 'ep')), may hold values from -6 to 6
- o_weight: bfloat16 [8192, 2048], P('ep'), may hold values from -0.0625 to 0.0625
- norm_gain: float32 [2048], replicated, may hold values from 0.5 to 1.5
- expert_gate_up: bfloat16 [128, 2048, 1536], P(('dp', 'ep')), may hold values from -0.125 to 0.125
- expert_down: bfloat16 [128, 768, 2048], P(('dp', 'ep')), may hold values from -0.21875 to 0.21875
- routes: int32 [2048, 2, 8], P(('dp', 'ep')), may hold values from 0 to 127, all different within a row; in each aligned block of 32 rows (0 to 31, 32 to 63, ..., all dimensions but the last counted through in order) at most 4 rows name the same one
- route_weights: float32 [2048, 2, 8], P(('dp', 'ep')), may hold values from 0.05 to 0.5
Outputs:
- attended: bfloat16 [2048, 2, 8192], P(('dp', 'ep'))
- layer_out: bfloat16 [2048, 2, 2048], P(('dp', 'ep'))
The draws below stay inside these ranges and needn't reach their ends.
Inputs may be any that keep to these rules, and one draw needn't show every extreme that they name: `lengths`: the largest length is 510 in every draw. `routes`: each token names 8 different experts; among the rows of one device (32 tokens) no expert is named more than 4 times, a bound that some block reaches.
All inputs are finite; a program needn't handle non-finite values. No bound on the sum of `merge_flags` on one device may be relied on, other than what follows from the above.
Results may differ from the reference program's by a relative error of at most 0.018.
Values may be sent and summed in bfloat16 or wider, within the bound.
No kernel may reach another device: no remote copies, remote signals or barrier semaphores. Data moves between devices by JAX's collectives and lax.ppermute only.
A program may use at most 128 MiB of HBM per device.

```python
import math
import jax
import jax.numpy as jnp
import numpy as np
from jax import lax

D = 2048
QH = 64
KVH = 4
HD = 128
FF = 768
TOPK = 8
STEPS = 2
R_DEV = 16
CAP = 512
EXPERTS = 128
REQ = 2048
CAPE = 4
N_DP = 4
N_EP = 32


def first_keys(key):
    return jax.random.truncated_normal(jax.random.fold_in(key, 12), -5.0, 5.0, (REQ, KVH * HD), jnp.float32)


def draw_key_cache(key, part):
    rest = jax.random.truncated_normal(jax.random.fold_in(key, 13), -5.0, 5.0, (REQ, CAP, KVH * HD), jnp.float32)
    first = first_keys(key)
    rest = rest.at[:, 0].set(first)
    return rest.astype(jnp.bfloat16)


def draw_queries(key, part):
    base = jax.random.truncated_normal(jax.random.fold_in(key, 14), -5.0, 5.0, (REQ, STEPS, QH * HD), jnp.float32)
    return base.astype(jnp.bfloat16)


def draw_lengths(key, part):
    first, second, third, fourth = jax.random.split(key, 4)
    short_lengths = jax.random.randint(first, (REQ,), 2, max(3, CAP // 8))
    long_lengths = jax.random.randint(second, (REQ,), CAP // 2, CAP - STEPS + 1)
    picked = jax.random.randint(third, (REQ,), 0, 8) == 0
    result = jnp.where(picked, long_lengths, short_lengths)
    longest = jax.random.randint(fourth, (), 0, REQ)
    return result.at[longest].set(CAP - STEPS).astype(jnp.int32)


def plant(array, own_key, smallest, largest):
    dims = array.shape
    place = [jax.random.randint(jax.random.fold_in(own_key, axis), (), 0, dims[axis]) for axis in range(len(dims))]
    array = array.at[tuple(place)].set(smallest)
    longest = dims.index(max(dims))
    place[longest] = (place[longest] + 1) % dims[longest]
    return array.at[tuple(place)].set(largest)


def levels(stream_key, extent, cuts, least, top_value):
    def one(position, parts):
        steps = jax.random.uniform(jax.random.fold_in(jax.random.fold_in(stream_key, 6), position), (parts,), jnp.float32, least / len(cuts), top_value / len(cuts))
        return jnp.repeat(jnp.exp(steps), extent[position] // parts).reshape((-1,) + (1,) * (len(extent) - position - 1))

    gain = one(*cuts[0])
    for cut in cuts[1:]:
        gain = gain * one(*cut)
    return gain


def shared_out(rng, own, number, rows, count, top, reach, lean):
    order = jax.random.permutation(rng, count)
    heavy_load, usual = portions_of(count, rows * top, reach, lean, True), portions_of(count, rows * top, reach, lean, False)
    places = jnp.arange(count)

    def named(sizes, turn):
        used = int((sizes > 0).sum())
        fixed = max(1, used // 4)
        moved = fixed + (places - fixed + turn * (used - fixed)) % max(1, count - fixed)
        return jnp.zeros((count,), jnp.int32).at[order[jnp.where(places < fixed, places, moved)]].set(jnp.asarray(sizes, jnp.int32))

    sizes = jnp.where(number % 4 == 0, named(heavy_load, number // 4), named(usual, number - number // 4 - 1))
    mixed = jax.random.permutation(jax.random.fold_in(own, 3), count)
    giver, receiver = mixed[0:count // 2 * 2:2], mixed[1:count // 2 * 2:2]
    margin = jnp.minimum(sizes[giver] - 1, reach - sizes[receiver]) // 2
    margin = jnp.where((giver == order[0]) | (receiver == order[0]) | (sizes[receiver] == 0), 0, jnp.maximum(margin, 0))
    moved = jax.random.randint(jax.random.fold_in(own, 4), (count // 2,), 0, 1 << 20) % (margin + 1)
    sizes = sizes.at[giver].add(-moved).at[receiver].add(moved)
    members = jnp.searchsorted(jnp.cumsum(sizes), jnp.arange(rows * top), side="right").astype(jnp.int32)
    grid = members.reshape(top, rows).T
    grid = grid[jax.random.permutation(jax.random.fold_in(own, 1), rows)]
    turn = jax.random.randint(jax.random.fold_in(own, 2), (rows, 1), 0, top)
    return jnp.take_along_axis(grid, (jnp.arange(top)[None, :] + turn) % top, axis=1)


def portions_of(count, total, reach, slope, full):
    loads = [(1 << 20) // math.isqrt(rank ** slope) + 1 for rank in range(1, count + 1)]
    largest = reach if full else min(reach, max(-(-total // count), total * loads[0] // sum(loads)))
    least = 1 if total - largest >= count - 1 else 0
    given, spare = [largest] + [least] * (count - 1), total - largest - least * (count - 1)
    while spare > 0:
        movable = [i for i in range(1, count) if given[i] < largest] or [i for i in range(1, count) if given[i] < reach]
        pool, left = sum([loads[i] for i in movable]), spare
        for i in movable:
            more = min(reach - given[i], max(1, left * loads[i] // pool), spare)
            given[i] = given[i] + more
            spare = spare - more
    return np.array(given)


def scatter_about(key, shape, width, reach, shards=(), kind=jnp.bfloat16):
    values = jax.random.normal(key, shape, jnp.float32) * width
    if len(shards) > 0:
        values = levels(key, shape, shards, -0.22, 0.18) * values
    return jnp.clip(values, min=-reach, max=reach).astype(kind)


def setup_inputs(seed: int = 0) -> dict:
    seeds = jax.random.split(jax.random.key(seed), 17)
    queries = draw_queries(jax.random.fold_in(seeds[16], 71), 0)
    keys_new = scatter_about(seeds[1], (REQ, STEPS, KVH * HD), 1.0, 5.0, ((0, 128),))
    values_new = scatter_about(seeds[2], (REQ, STEPS, KVH * HD), 1.0, 5.0, ((0, 128),))
    importance = jnp.clip(jnp.exp(math.log(4.0) - 2.7725887 * jax.random.uniform(seeds[3], (REQ, STEPS, KVH), jnp.float32) ** levels(seeds[3], (REQ, STEPS, KVH), ((0, 128),), -0.2, 0.2)), 0.25, 4.0)
    merge_flags = plant((jax.random.randint(seeds[4], (REQ, STEPS, KVH), 0, 4) < 3).astype(jnp.int32), jax.random.fold_in(seeds[4], 1), 0, 1)
    key_cache = draw_key_cache(jax.random.fold_in(seeds[16], 71), 0)
    value_cache = scatter_about(seeds[6], (REQ, CAP, KVH * HD), 1.0, 5.0, ((0, 128),))
    last_weight = jnp.clip(jnp.exp(math.log(8.0) - 2.7725887 * jax.random.uniform(seeds[7], (REQ, KVH), jnp.float32) ** levels(seeds[7], (REQ, KVH), ((0, 128),), -0.2, 0.2)), 0.5, 8.0)
    lengths = draw_lengths(jax.random.fold_in(seeds[16], 71), 0)
    residual = scatter_about(seeds[9], (REQ, STEPS, D), 1.0, 6.0, ((0, 128),))
    o_weight = scatter_about(seeds[10], (QH * HD, D), (QH * HD) ** -0.5, 0.0625, ((0, 32),))
    norm_gain = jnp.clip(1.0 + 0.1 * jax.random.normal(seeds[11], (D,), jnp.float32), 0.5, 1.5)
    expert_gate_up = scatter_about(seeds[12], (EXPERTS, D, 2 * FF), D ** -0.5, 0.125, ((0, 128),))
    expert_down = scatter_about(seeds[13], (EXPERTS, FF, D), FF ** -0.5, 0.21875, ((0, 128),))
    routes_keys = jax.random.split(jax.random.fold_in(seeds[14], 1), REQ * STEPS // (R_DEV * STEPS))
    routes_turns = jax.random.permutation(jax.random.fold_in(seeds[14], 3), REQ * STEPS // (R_DEV * STEPS))
    routes = jax.vmap(lambda own, number: shared_out(jax.random.fold_in(seeds[14], 2), own, number, R_DEV * STEPS, EXPERTS, TOPK, CAPE, 2))(routes_keys, routes_turns).reshape((REQ, STEPS, TOPK))
    route_weights = jnp.clip(jnp.exp(math.log(0.5) - 2.3025851 * jax.random.uniform(seeds[15], (REQ, STEPS, TOPK), jnp.float32) ** levels(seeds[15], (REQ, STEPS, TOPK), ((0, 128),), -0.2, 0.2)), 0.05, 0.5)
    return dict(queries=queries, keys_new=keys_new, values_new=values_new, importance=importance, merge_flags=merge_flags, key_cache=key_cache, value_cache=value_cache, last_weight=last_weight, lengths=lengths, residual=residual, o_weight=o_weight, norm_gain=norm_gain, expert_gate_up=expert_gate_up, expert_down=expert_down, routes=routes, route_weights=route_weights)


EPS = 1e-06

def one_request(query_rows, fresh_keys, fresh_values, shares, flags, key_rows, value_rows, weight, length):
    group = QH // KVH
    scale = 1.0 / jnp.sqrt(jnp.float32(HD))
    keys = key_rows.reshape(CAP, KVH, HD)
    values = value_rows.reshape(CAP, KVH, HD)
    count = jnp.full((KVH,), length, dtype=jnp.int32)
    heads = jnp.arange(KVH, dtype=jnp.int32)
    slots = jnp.arange(CAP, dtype=jnp.int32)
    outputs = []
    for step in range(STEPS):
        merging = flags[step] == 1
        share = shares[step]
        target = jnp.where(merging, count - 1, count).astype(jnp.int32)
        new_keys = fresh_keys[step].reshape(KVH, HD).astype(jnp.float32)
        new_values = fresh_values[step].reshape(KVH, HD).astype(jnp.float32)
        old_keys = keys[target, heads].astype(jnp.float32)
        old_values = values[target, heads].astype(jnp.float32)
        mixed_keys = (weight[:, None] * old_keys + share[:, None] * new_keys) / (weight + share)[:, None]
        mixed_values = (weight[:, None] * old_values + share[:, None] * new_values) / (weight + share)[:, None]
        keys = keys.at[target, heads].set(jnp.where(merging[:, None], mixed_keys, new_keys).astype(jnp.bfloat16))
        values = values.at[target, heads].set(jnp.where(merging[:, None], mixed_values, new_values).astype(jnp.bfloat16))
        weight = jnp.where(merging, weight + share, share)
        count = jnp.where(merging, count, count + 1)
        query = query_rows[step].reshape(KVH, group, HD).astype(jnp.float32)
        score = jnp.einsum('gqd,kgd->gqk', query, keys.astype(jnp.float32)) * scale
        score = jnp.where(slots[None, None, :] < count[:, None, None], score, -jnp.inf)
        highest = lax.optimization_barrier(jnp.max(score, axis=2, keepdims=True))
        raw = jnp.exp(score - highest)
        total = lax.optimization_barrier(jnp.sum(raw, axis=2, keepdims=True))
        rounded = lax.optimization_barrier(raw.astype(jnp.bfloat16)).astype(jnp.float32)
        result = jnp.einsum('gqk,kgd->gqd', rounded, values.astype(jnp.float32)) / total
        outputs.append(result.astype(jnp.bfloat16).reshape(QH * HD))
    return jnp.stack(outputs)

def reference(queries, keys_new, values_new, importance, merge_flags, key_cache, value_cache, last_weight, lengths, residual, o_weight, norm_gain, expert_gate_up, expert_down, routes, route_weights):
    attended = lax.map(lambda pack: one_request(*pack), (queries, keys_new, values_new, importance, merge_flags, key_cache, value_cache, last_weight, lengths))
    rows = REQ * STEPS
    projected = jnp.dot(attended.reshape(rows, QH * HD), o_weight, preferred_element_type=jnp.float32)
    mixed = residual.reshape(rows, D).astype(jnp.float32) + projected
    normed = (mixed * lax.rsqrt(lax.optimization_barrier(jnp.mean(mixed * mixed, axis=1, keepdims=True)) + EPS) * norm_gain).astype(jnp.bfloat16)
    chosen = routes.reshape(rows, TOPK)
    gates = route_weights.reshape(rows, TOPK)
    most = CAPE * N_DP * N_EP

    def one_expert(blended, expert):
        hits = chosen == expert
        gate = lax.optimization_barrier(jnp.sum(jnp.where(hits, gates, 0.0), axis=1))
        member = jnp.any(hits, axis=1)
        picked = jnp.nonzero(member, size=most, fill_value=0)[0].astype(jnp.int32)
        valid = jnp.arange(most, dtype=jnp.int32) < jnp.sum(member.astype(jnp.int32))
        inputs = normed[picked]
        both = jnp.dot(inputs, expert_gate_up[expert], preferred_element_type=jnp.float32)
        active = (jax.nn.silu(both[:, :FF]) * both[:, FF:]).astype(jnp.bfloat16)
        output = jnp.dot(active, expert_down[expert], preferred_element_type=jnp.float32).astype(jnp.bfloat16)
        term = jnp.where(valid[:, None], gate[picked][:, None] * output.astype(jnp.float32), 0.0)
        return (blended.at[picked].add(term), expert)
    blended, unused = lax.scan(one_expert, jnp.zeros((rows, D), jnp.float32), jnp.arange(EXPERTS, dtype=jnp.int32))
    layer_out = (mixed + blended).astype(jnp.bfloat16).reshape(REQ, STEPS, D)
    return (attended, layer_out)
```

```python
import math

import jax
import jax.numpy as jnp
from jax import lax
from jax.sharding import PartitionSpec as P

EPS = 1e-06


def build_tail(
    key_cache,
    value_cache,
    lengths,
    keys_new,
    values_new,
    importance,
    merge_flags,
    last_weight,
    heads_kv,
):
    requests, steps, features = keys_new.shape
    head_dim = features // heads_kv
    last_slot = lengths - 1

    def take_slot(cache_rows, position):
        return lax.dynamic_slice_in_dim(cache_rows, position, 1, 0)

    first_keys = jax.vmap(take_slot)(key_cache, last_slot)
    first_values = jax.vmap(take_slot)(value_cache, last_slot)
    blank = jnp.zeros((requests, steps, features), jnp.bfloat16)
    tail_keys = jnp.concatenate([first_keys, blank], axis=1).reshape(
        requests, steps + 1, heads_kv, head_dim
    )
    tail_values = jnp.concatenate([first_values, blank], axis=1).reshape(
        requests, steps + 1, heads_kv, head_dim
    )
    filled = jnp.ones((requests, heads_kv), jnp.int32)
    weight = last_weight
    positions = jnp.arange(steps + 1, dtype=jnp.int32)
    live_counts = []
    key_states = []
    value_states = []
    for step in range(steps):
        merging = merge_flags[:, step] == 1
        portion = importance[:, step]
        target = jnp.where(merging, filled - 1, filled)
        picked = positions[None, :, None] == target[:, None, :]

        def settle(tail, fresh):
            fresh = fresh.reshape(requests, heads_kv, head_dim).astype(jnp.float32)
            former = jnp.sum(jnp.where(picked[..., None], tail.astype(jnp.float32), 0.0), axis=1)
            blended = (weight[..., None] * former + portion[..., None] * fresh) / (
                weight + portion
            )[..., None]
            new_row = jnp.where(merging[..., None], blended, fresh).astype(jnp.bfloat16)
            return jnp.where(picked[..., None], new_row[:, None], tail)

        tail_keys = settle(tail_keys, keys_new[:, step])
        tail_values = settle(tail_values, values_new[:, step])
        weight = jnp.where(merging, weight + portion, portion)
        filled = jnp.where(merging, filled, filled + 1)
        live_counts.append(filled)
        key_states.append(tail_keys)
        value_states.append(tail_values)
    return (
        jnp.stack(key_states, axis=1),
        jnp.stack(value_states, axis=1),
        jnp.stack(live_counts, axis=2),
    )


def first_pass(keys, queries, slot_order, limits, block, scale):
    requests, slots = (keys.shape[0], keys.shape[1])
    heads_kv, rows = (queries.shape[1], queries.shape[2])
    usable = jnp.sum((slot_order[None, :] < limits[:, None]).astype(jnp.int32), axis=1)
    blocks = (jnp.max(usable) + block - 1) // block
    initial = jnp.full((requests, heads_kv, rows, slots), -jnp.inf, jnp.float32)

    def first_advance(index, buffer):
        start = index * block
        key_block = lax.dynamic_slice_in_dim(keys, start, block, 1)
        scores = (
            jnp.einsum("ngqd,nkgd->ngqk", queries, key_block, preferred_element_type=jnp.float32)
            * scale
        )
        order_block = lax.dynamic_slice_in_dim(slot_order, start, block, 0)
        valid = order_block[None, :] < limits[:, None]
        scores = jnp.where(valid[:, None, None, :], scores, -jnp.inf)
        return lax.dynamic_update_slice_in_dim(buffer, scores, start, 3)

    return (lax.fori_loop(0, blocks, first_advance, initial), blocks)


def second_pass(values, buffer, highest, blocks, block):
    requests, heads_kv, rows = (buffer.shape[0], buffer.shape[1], buffer.shape[2])
    head_dim = values.shape[3]

    def second_advance(index, carry):
        summed, totals = carry
        start = index * block
        scores = lax.dynamic_slice_in_dim(buffer, start, block, 3)
        raw = jnp.exp(scores - highest[..., None])
        totals = totals + jnp.sum(raw, axis=3)
        value_block = lax.dynamic_slice_in_dim(values, start, block, 1)
        summed = summed + jnp.einsum(
            "ngqk,nkgd->ngqd",
            raw.astype(jnp.bfloat16),
            value_block,
            preferred_element_type=jnp.float32,
        )
        return (summed, totals)

    initial = (
        jnp.zeros((requests, heads_kv, rows, head_dim), jnp.float32),
        jnp.zeros((requests, heads_kv, rows), jnp.float32),
    )
    return lax.fori_loop(0, blocks, second_advance, initial)


def run_experts(arriving, expert_gate_up, expert_down):
    hidden_units = expert_down.shape[1]
    both = jnp.einsum(
        "sjcd,jdf->sjcf", arriving, expert_gate_up, preferred_element_type=jnp.float32
    )
    active = (jax.nn.silu(both[..., :hidden_units]) * both[..., hidden_units:]).astype(jnp.bfloat16)
    return jnp.einsum(
        "sjcf,jfd->sjcd", active, expert_down, preferred_element_type=jnp.float32
    ).astype(jnp.bfloat16)


def shards(
    queries,
    keys_new,
    values_new,
    importance,
    merge_flags,
    key_cache,
    value_cache,
    last_weight,
    lengths,
    residual,
    o_weight,
    norm_gain,
    expert_gate_up,
    expert_down,
    routes,
    route_weights,
):
    heads_kv = last_weight.shape[1]
    requests, steps, query_width = queries.shape
    features = keys_new.shape[2]
    head_dim = features // heads_kv
    heads_query = query_width // head_dim
    group = heads_query // heads_kv
    slots_all = key_cache.shape[1]
    scale = 1.0 / math.sqrt(head_dim)
    tail_keys, tail_values, live = build_tail(
        key_cache,
        value_cache,
        lengths,
        keys_new,
        values_new,
        importance,
        merge_flags,
        last_weight,
        heads_kv,
    )
    grouped = (
        queries.reshape(requests, steps, heads_kv, group, head_dim)
        .transpose(0, 2, 1, 3, 4)
        .reshape(requests, heads_kv, steps * group, head_dim)
    )
    per_step = grouped.reshape(requests, heads_kv, steps, group, head_dim)
    tail_scores = (
        jnp.einsum("ngtqd,ntsgd->ngtqs", per_step, tail_keys, preferred_element_type=jnp.float32)
        * scale
    )
    tail_scores = tail_scores.reshape(requests, heads_kv, steps * group, steps + 1)
    live_rows = jnp.repeat(live, group, axis=2)
    tail_valid = jnp.arange(steps + 1, dtype=jnp.int32)[None, None, None, :] < live_rows[..., None]
    tail_scores = jnp.where(tail_valid, tail_scores, -jnp.inf)
    tail_highest = jnp.max(tail_scores, axis=3)
    limits = lengths - 1
    keys_grid = key_cache.reshape(requests, slots_all, heads_kv, head_dim)
    values_grid = value_cache.reshape(requests, slots_all, heads_kv, head_dim)
    block = math.gcd(slots_all, 256)
    slot_order = jnp.arange(slots_all, dtype=jnp.int32)
    buffer, blocks = first_pass(keys_grid, grouped, slot_order, limits, block, scale)
    highest = jnp.maximum(jnp.max(buffer, axis=3), tail_highest)
    summed, totals = second_pass(values_grid, buffer, highest, blocks, block)
    tail_raw = jnp.exp(tail_scores - highest[..., None])
    totals = totals + jnp.sum(tail_raw, axis=3)
    tail_weights = tail_raw.astype(jnp.bfloat16).reshape(
        requests, heads_kv, steps, group, steps + 1
    )
    tail_sums = jnp.einsum(
        "ngtqs,ntsgd->ngtqd", tail_weights, tail_values, preferred_element_type=jnp.float32
    )
    summed = summed + tail_sums.reshape(requests, heads_kv, steps * group, head_dim)
    attended = (summed / totals[..., None]).astype(jnp.bfloat16)
    attended = (
        attended.reshape(requests, heads_kv, steps, group, head_dim)
        .transpose(0, 2, 1, 3, 4)
        .reshape(requests, steps, query_width)
    )
    rows = requests * steps
    width = o_weight.shape[1]
    gathered = lax.all_gather(o_weight, ("x", "c"), axis=0, tiled=True)
    lines = lax.axis_size("y")
    spread = lax.all_to_all(
        attended.reshape(rows, lines, query_width // lines),
        "y",
        split_axis=1,
        concat_axis=0,
        tiled=True,
    )
    spread = spread.reshape(lines * rows, query_width // lines)
    projected = lax.psum_scatter(
        jnp.dot(spread, gathered, preferred_element_type=jnp.float32),
        "y",
        scatter_dimension=0,
        tiled=True,
    )
    members = lax.axis_size("y") * lax.axis_size("x") * lax.axis_size("c")
    mixed = residual.reshape(rows, width).astype(jnp.float32) + projected
    normed = (
        mixed * lax.rsqrt(jnp.mean(mixed * mixed, axis=1, keepdims=True) + EPS) * norm_gain
    ).astype(jnp.bfloat16)
    experts_local = expert_gate_up.shape[0]
    dp_size = lax.axis_size("dp")
    experts_all = experts_local * dp_size * members
    top_k = routes.shape[2]
    capacity = max(2, 2 * rows * top_k // experts_all)
    chosen = routes.reshape(rows * top_k)
    sequence = jnp.arange(rows * top_k, dtype=jnp.int32)
    earlier = sequence[:, None] > sequence[None, :]
    rank = jnp.sum(((chosen[:, None] == chosen[None, :]) & earlier).astype(jnp.int32), axis=1)
    target = chosen * capacity + rank
    placing = (
        jnp.arange(experts_all * capacity, dtype=jnp.int32)[:, None] == target[None, :]
    ).reshape(experts_all * capacity, rows, top_k)
    placing = jnp.any(placing, axis=2).astype(jnp.bfloat16)
    outgoing = jnp.dot(placing, normed, preferred_element_type=jnp.float32).astype(jnp.bfloat16)
    arrived = lax.all_to_all(
        outgoing.reshape(experts_all, capacity, width),
        ("dp", "y", "x", "c"),
        split_axis=0,
        concat_axis=0,
        tiled=True,
    )
    depth = arrived.shape[1]
    sources = arrived.shape[0] // experts_local
    answer = run_experts(
        arrived.reshape(sources, experts_local, depth, width), expert_gate_up, expert_down
    )
    returned = lax.all_to_all(
        answer.reshape(sources * experts_local, depth, width),
        ("dp", "y", "x", "c"),
        split_axis=0,
        concat_axis=0,
        tiled=True,
    )
    results = returned.reshape(experts_all * capacity, width)[target].reshape(rows, top_k, width)
    blended = jnp.sum(route_weights.reshape(rows, top_k, 1) * results.astype(jnp.float32), axis=1)
    layer_out = (mixed + blended).astype(jnp.bfloat16).reshape(requests, steps, width)
    return (attended, layer_out)


def solution(mesh):
    lines = mesh.devices.shape[1] // 8
    mesh = jax.sharding.Mesh(
        mesh.devices.reshape(mesh.devices.shape[0], lines, 4, 2), ("dp", "y", "x", "c")
    )
    return jax.shard_map(
        shards,
        mesh=mesh,
        in_specs=(
            P(("dp", "y", "x", "c"), None, None),
            P(("dp", "y", "x", "c"), None, None),
            P(("dp", "y", "x", "c"), None, None),
            P(("dp", "y", "x", "c"), None, None),
            P(("dp", "y", "x", "c"), None, None),
            P(("dp", "y", "x", "c"), None, None),
            P(("dp", "y", "x", "c"), None, None),
            P(("dp", "y", "x", "c"), None),
            P(("dp", "y", "x", "c")),
            P(("dp", "y", "x", "c"), None, None),
            P(("y", "x", "c"), None),
            P(),
            P(("dp", "y", "x", "c"), None, None),
            P(("dp", "y", "x", "c"), None, None),
            P(("dp", "y", "x", "c"), None, None),
            P(("dp", "y", "x", "c"), None, None),
        ),
        out_specs=(P(("dp", "y", "x", "c"), None, None), P(("dp", "y", "x", "c"), None, None)),
        check_vma=False,
    )
```

```python
import math

import jax
import jax.numpy as jnp
from jax import lax
from jax.experimental import pallas as pl
from jax.experimental.pallas import tpu as pltpu
from jax.sharding import PartitionSpec as P

EPS = 1e-06


def build_tail(
    key_cache,
    value_cache,
    lengths,
    keys_new,
    values_new,
    importance,
    merge_flags,
    last_weight,
    heads_kv,
):
    requests, steps, features = keys_new.shape
    head_dim = features // heads_kv
    last_slot = lengths - 1

    def take_slot(cache_rows, position):
        return lax.dynamic_slice_in_dim(cache_rows, position, 1, 0)

    first_keys = jax.vmap(take_slot)(key_cache, last_slot)
    first_values = jax.vmap(take_slot)(value_cache, last_slot)
    blank = jnp.zeros((requests, steps, features), jnp.bfloat16)
    tail_keys = jnp.concatenate([first_keys, blank], axis=1).reshape(
        requests, steps + 1, heads_kv, head_dim
    )
    tail_values = jnp.concatenate([first_values, blank], axis=1).reshape(
        requests, steps + 1, heads_kv, head_dim
    )
    filled = jnp.ones((requests, heads_kv), jnp.int32)
    weight = last_weight
    positions = jnp.arange(steps + 1, dtype=jnp.int32)
    live_counts = []
    key_states = []
    value_states = []
    for step in range(steps):
        merging = merge_flags[:, step] == 1
        portion = importance[:, step]
        target = jnp.where(merging, filled - 1, filled)
        picked = positions[None, :, None] == target[:, None, :]

        def settle(tail, fresh):
            fresh = fresh.reshape(requests, heads_kv, head_dim).astype(jnp.float32)
            former = jnp.sum(jnp.where(picked[..., None], tail.astype(jnp.float32), 0.0), axis=1)
            blended = (weight[..., None] * former + portion[..., None] * fresh) / (
                weight + portion
            )[..., None]
            new_row = jnp.where(merging[..., None], blended, fresh).astype(jnp.bfloat16)
            return jnp.where(picked[..., None], new_row[:, None], tail)

        tail_keys = settle(tail_keys, keys_new[:, step])
        tail_values = settle(tail_values, values_new[:, step])
        weight = jnp.where(merging, weight + portion, portion)
        filled = jnp.where(merging, filled, filled + 1)
        live_counts.append(filled)
        key_states.append(tail_keys)
        value_states.append(tail_values)
    return (
        jnp.stack(key_states, axis=1),
        jnp.stack(value_states, axis=1),
        jnp.stack(live_counts, axis=2),
    )


def cache_attention(grouped, key_cache, value_cache, limits, tail_highest, scale):
    requests, heads_kv, rows, head_dim = grouped.shape
    slots, width = key_cache.shape[1], key_cache.shape[2]

    def kernel(limit_ref, q_ref, k_ref, v_ref, th_ref, acc_ref, tot_ref, top_ref):
        limit = limit_ref[pl.program_id(0)]
        valid = lax.broadcasted_iota(jnp.int32, (rows, slots), 1) < limit
        for g in range(heads_kv):
            lanes = slice(g * head_dim, (g + 1) * head_dim)
            scores = (
                lax.dot_general(
                    q_ref[0, g],
                    k_ref[0, :, lanes],
                    (((1,), (1,)), ((), ())),
                    preferred_element_type=jnp.float32,
                )
                * scale
            )
            scores = jnp.where(valid, scores, -jnp.inf)
            top = jnp.maximum(jnp.max(scores, axis=1, keepdims=True), th_ref[0, g])
            raw = jnp.exp(scores - top)
            tot_ref[0, g] = jnp.sum(raw, axis=1, keepdims=True)
            top_ref[0, g] = top
            acc_ref[0, g] = jnp.dot(
                raw.astype(jnp.bfloat16), v_ref[0, :, lanes], preferred_element_type=jnp.float32
            )

    per_row = pl.BlockSpec((1, heads_kv, rows, head_dim), lambda r, lim: (r, 0, 0, 0))
    per_head = pl.BlockSpec((1, heads_kv, rows, 1), lambda r, lim: (r, 0, 0, 0))
    per_cache = pl.BlockSpec((1, slots, width), lambda r, lim: (r, 0, 0))
    return pl.pallas_call(
        kernel,
        out_shape=(
            jax.ShapeDtypeStruct((requests, heads_kv, rows, head_dim), jnp.float32),
            jax.ShapeDtypeStruct((requests, heads_kv, rows, 1), jnp.float32),
            jax.ShapeDtypeStruct((requests, heads_kv, rows, 1), jnp.float32),
        ),
        grid_spec=pltpu.PrefetchScalarGridSpec(
            num_scalar_prefetch=1,
            grid=(requests,),
            in_specs=[per_row, per_cache, per_cache, per_head],
            out_specs=[per_row, per_head, per_head],
        ),
    )(limits, grouped, key_cache, value_cache, tail_highest)

def run_experts(arriving, expert_gate_up, expert_down):
    hidden_units = expert_down.shape[1]
    both = jnp.einsum(
        "sjcd,jdf->sjcf", arriving, expert_gate_up, preferred_element_type=jnp.float32
    )
    active = (jax.nn.silu(both[..., :hidden_units]) * both[..., hidden_units:]).astype(jnp.bfloat16)
    return jnp.einsum(
        "sjcf,jfd->sjcd", active, expert_down, preferred_element_type=jnp.float32
    ).astype(jnp.bfloat16)


def shards(
    queries,
    keys_new,
    values_new,
    importance,
    merge_flags,
    key_cache,
    value_cache,
    last_weight,
    lengths,
    residual,
    o_weight,
    norm_gain,
    expert_gate_up,
    expert_down,
    routes,
    route_weights,
):
    heads_kv = last_weight.shape[1]
    requests, steps, query_width = queries.shape
    features = keys_new.shape[2]
    head_dim = features // heads_kv
    heads_query = query_width // head_dim
    group = heads_query // heads_kv
    slots_all = key_cache.shape[1]
    scale = 1.0 / math.sqrt(head_dim)
    tail_keys, tail_values, live = build_tail(
        key_cache,
        value_cache,
        lengths,
        keys_new,
        values_new,
        importance,
        merge_flags,
        last_weight,
        heads_kv,
    )
    grouped = (
        queries.reshape(requests, steps, heads_kv, group, head_dim)
        .transpose(0, 2, 1, 3, 4)
        .reshape(requests, heads_kv, steps * group, head_dim)
    )
    per_step = grouped.reshape(requests, heads_kv, steps, group, head_dim)
    tail_scores = (
        jnp.einsum("ngtqd,ntsgd->ngtqs", per_step, tail_keys, preferred_element_type=jnp.float32)
        * scale
    )
    tail_scores = tail_scores.reshape(requests, heads_kv, steps * group, steps + 1)
    live_rows = jnp.repeat(live, group, axis=2)
    tail_valid = jnp.arange(steps + 1, dtype=jnp.int32)[None, None, None, :] < live_rows[..., None]
    tail_scores = jnp.where(tail_valid, tail_scores, -jnp.inf)
    tail_highest = jnp.max(tail_scores, axis=3)
    limits = lengths - 1
    summed, totals, highest = cache_attention(
        grouped, key_cache, value_cache, limits, tail_highest[..., None], scale
    )
    totals = totals[..., 0]
    highest = highest[..., 0]
    tail_raw = jnp.exp(tail_scores - highest[..., None])
    totals = totals + jnp.sum(tail_raw, axis=3)
    tail_weights = tail_raw.astype(jnp.bfloat16).reshape(
        requests, heads_kv, steps, group, steps + 1
    )
    tail_sums = jnp.einsum(
        "ngtqs,ntsgd->ngtqd", tail_weights, tail_values, preferred_element_type=jnp.float32
    )
    summed = summed + tail_sums.reshape(requests, heads_kv, steps * group, head_dim)
    attended = (summed / totals[..., None]).astype(jnp.bfloat16)
    attended = (
        attended.reshape(requests, heads_kv, steps, group, head_dim)
        .transpose(0, 2, 1, 3, 4)
        .reshape(requests, steps, query_width)
    )
    rows = requests * steps
    width = o_weight.shape[1]
    gathered = lax.all_gather(o_weight, ("x", "c"), axis=0, tiled=True)
    lines = lax.axis_size("y")
    spread = lax.all_to_all(
        attended.reshape(rows, lines, query_width // lines),
        "y",
        split_axis=1,
        concat_axis=0,
        tiled=True,
    )
    spread = spread.reshape(lines * rows, query_width // lines)
    projected = lax.psum_scatter(
        jnp.dot(spread, gathered, preferred_element_type=jnp.float32),
        "y",
        scatter_dimension=0,
        tiled=True,
    )
    members = lax.axis_size("y") * lax.axis_size("x") * lax.axis_size("c")
    mixed = residual.reshape(rows, width).astype(jnp.float32) + projected
    normed = (
        mixed * lax.rsqrt(jnp.mean(mixed * mixed, axis=1, keepdims=True) + EPS) * norm_gain
    ).astype(jnp.bfloat16)
    experts_local = expert_gate_up.shape[0]
    dp_size = lax.axis_size("dp")
    experts_all = experts_local * dp_size * members
    top_k = routes.shape[2]
    capacity = max(2, 2 * rows * top_k // experts_all)
    chosen = routes.reshape(rows * top_k)
    sequence = jnp.arange(rows * top_k, dtype=jnp.int32)
    earlier = sequence[:, None] > sequence[None, :]
    rank = jnp.sum(((chosen[:, None] == chosen[None, :]) & earlier).astype(jnp.int32), axis=1)
    target = chosen * capacity + rank
    placing = (
        jnp.arange(experts_all * capacity, dtype=jnp.int32)[:, None] == target[None, :]
    ).reshape(experts_all * capacity, rows, top_k)
    placing = jnp.any(placing, axis=2).astype(jnp.bfloat16)
    outgoing = jnp.dot(placing, normed, preferred_element_type=jnp.float32).astype(jnp.bfloat16)
    arrived = lax.all_to_all(
        outgoing.reshape(experts_all, capacity, width),
        ("dp", "y", "x", "c"),
        split_axis=0,
        concat_axis=0,
        tiled=True,
    )
    depth = arrived.shape[1]
    sources = arrived.shape[0] // experts_local
    answer = run_experts(
        arrived.reshape(sources, experts_local, depth, width), expert_gate_up, expert_down
    )
    returned = lax.all_to_all(
        answer.reshape(sources * experts_local, depth, width),
        ("dp", "y", "x", "c"),
        split_axis=0,
        concat_axis=0,
        tiled=True,
    )
    results = returned.reshape(experts_all * capacity, width)[target].reshape(rows, top_k, width)
    blended = jnp.sum(route_weights.reshape(rows, top_k, 1) * results.astype(jnp.float32), axis=1)
    layer_out = (mixed + blended).astype(jnp.bfloat16).reshape(requests, steps, width)
    return (attended, layer_out)


def solution(mesh):
    lines = mesh.devices.shape[1] // 8
    mesh = jax.sharding.Mesh(
        mesh.devices.reshape(mesh.devices.shape[0], lines, 4, 2), ("dp", "y", "x", "c")
    )
    return jax.shard_map(
        shards,
        mesh=mesh,
        in_specs=(
            P(("dp", "y", "x", "c"), None, None),
            P(("dp", "y", "x", "c"), None, None),
            P(("dp", "y", "x", "c"), None, None),
            P(("dp", "y", "x", "c"), None, None),
            P(("dp", "y", "x", "c"), None, None),
            P(("dp", "y", "x", "c"), None, None),
            P(("dp", "y", "x", "c"), None, None),
            P(("dp", "y", "x", "c"), None),
            P(("dp", "y", "x", "c")),
            P(("dp", "y", "x", "c"), None, None),
            P(("y", "x", "c"), None),
            P(),
            P(("dp", "y", "x", "c"), None, None),
            P(("dp", "y", "x", "c"), None, None),
            P(("dp", "y", "x", "c"), None, None),
            P(("dp", "y", "x", "c"), None, None),
        ),
        out_specs=(P(("dp", "y", "x", "c"), None, None), P(("dp", "y", "x", "c"), None, None)),
        check_vma=False,
    )
```

```python
import math

import jax
import jax.numpy as jnp
from jax import lax
from jax.experimental import pallas as pl
from jax.experimental.pallas import tpu as pltpu
from jax.sharding import PartitionSpec as P

EPS = 1e-06


def decode_attention(queries, keys_new, values_new, importance, merge_flags, key_cache,
                     value_cache, last_weight, lengths):
    requests, steps, query_width = queries.shape
    heads_kv = last_weight.shape[1]
    slots, features = key_cache.shape[1], key_cache.shape[2]
    head_dim = features // heads_kv
    group = query_width // head_dim // heads_kv
    scale = 1.0 / math.sqrt(head_dim)
    f32, bf16 = jnp.float32, jnp.bfloat16

    def kernel(len_ref, flag_ref, share_ref, weight_ref, q_ref, kn_ref, vn_ref, k_ref, v_ref, o_ref):
        r = pl.program_id(0)
        n = len_ref[r]
        main_valid = lax.broadcasted_iota(jnp.int32, (group, slots), 1) < n - 1
        pick = (lax.broadcasted_iota(jnp.int32, (8, slots), 1) == n - 1).astype(bf16)
        last_k = jnp.dot(pick, k_ref[0], preferred_element_type=f32)[0:1]
        last_v = jnp.dot(pick, v_ref[0], preferred_element_type=f32)[0:1]
        new_k = kn_ref[0].astype(f32)
        new_v = vn_ref[0].astype(f32)

        def lane_mask(flag):
            return jnp.full((1, head_dim), flag, jnp.int32) == 1

        def row_mask(flag):
            return jnp.full((group, 1), flag, jnp.int32) == 1

        for g in range(heads_kv):
            lanes = slice(g * head_dim, (g + 1) * head_dim)
            z = weight_ref[r * heads_kv + g]
            f0 = flag_ref[(r * steps) * heads_kv + g]
            f1 = flag_ref[(r * steps + 1) * heads_kv + g]
            w0 = share_ref[(r * steps) * heads_kv + g]
            w1 = share_ref[(r * steps + 1) * heads_kv + g]
            z1 = jnp.where(f0 == 1, z + w0, w0)
            m0, m1 = lane_mask(f0), lane_mask(f1)
            both = lane_mask(f0 * f1)

            def settle(last, new):
                old0 = last[:, lanes]
                n0, n1 = new[0:1, lanes], new[1:2, lanes]
                b0 = ((z * old0 + w0 * n0) / (z + w0)).astype(bf16).astype(f32)
                a0 = jnp.where(m0, b0, old0)
                cur = jnp.where(m0, a0, n0)
                b1 = ((z1 * cur + w1 * n1) / (z1 + w1)).astype(bf16).astype(f32)
                second = (
                    jnp.where(both, b1, jnp.where(m0, a0, old0)),
                    jnp.where(m0, n1, jnp.where(m1, b1, n0)),
                    n1,
                )
                return (a0, n0), second

            keys_t = settle(last_k, new_k)
            values_t = settle(last_v, new_v)
            count0 = 2 - f0
            counts = (count0, count0 + 1 - f1)
            kg = k_ref[0, :, lanes]
            vg = v_ref[0, :, lanes]
            for t in range(steps):
                rows = slice(g * group, (g + 1) * group)
                q = q_ref[0, t, rows, :]
                main = (
                    lax.dot_general(q, kg, (((1,), (1,)), ((), ())), preferred_element_type=f32)
                    * scale
                )
                main = jnp.where(main_valid, main, -jnp.inf)
                qf = q.astype(f32)
                top = jnp.max(main, axis=1, keepdims=True)
                tails = []
                for j, (tk, tv) in enumerate(zip(keys_t[t], values_t[t])):
                    ts = jnp.sum(qf * tk, axis=1, keepdims=True) * scale
                    ts = jnp.where(row_mask((j < counts[t]).astype(jnp.int32)), ts, -jnp.inf)
                    top = jnp.maximum(top, ts)
                    tails.append((ts, tv))
                raw = jnp.exp(main - top)
                total = jnp.sum(raw, axis=1, keepdims=True)
                summed = jnp.dot(raw.astype(bf16), vg, preferred_element_type=f32)
                for ts, tv in tails:
                    part = jnp.exp(ts - top)
                    total = total + part
                    summed = summed + part.astype(bf16).astype(f32) * tv
                o_ref[0, t, rows, :] = (summed / total).astype(bf16)

    heads = query_width // head_dim
    per_query = pl.BlockSpec((1, steps, heads, head_dim), lambda r, *_: (r, 0, 0, 0))
    per_new = pl.BlockSpec((1, steps, features), lambda r, *_: (r, 0, 0))
    per_cache = pl.BlockSpec((1, slots, features), lambda r, *_: (r, 0, 0))
    out = pl.pallas_call(
        kernel,
        out_shape=jax.ShapeDtypeStruct((requests, steps, heads, head_dim), bf16),
        grid_spec=pltpu.PrefetchScalarGridSpec(
            num_scalar_prefetch=4,
            grid=(requests,),
            in_specs=[per_query, per_new, per_new, per_cache, per_cache],
            out_specs=per_query,
        ),
    )(
        lengths,
        merge_flags.reshape(-1),
        importance.reshape(-1),
        last_weight.reshape(-1),
        queries.reshape(requests, steps, heads, head_dim),
        keys_new,
        values_new,
        key_cache,
        value_cache,
    )
    return out.reshape(requests, steps, query_width)


def run_experts(arriving, expert_gate_up, expert_down):
    hidden_units = expert_down.shape[1]
    both = jnp.einsum(
        "sjcd,jdf->sjcf", arriving, expert_gate_up, preferred_element_type=jnp.float32
    )
    active = (jax.nn.silu(both[..., :hidden_units]) * both[..., hidden_units:]).astype(jnp.bfloat16)
    return jnp.einsum(
        "sjcf,jfd->sjcd", active, expert_down, preferred_element_type=jnp.float32
    ).astype(jnp.bfloat16)


def shards(
    queries,
    keys_new,
    values_new,
    importance,
    merge_flags,
    key_cache,
    value_cache,
    last_weight,
    lengths,
    residual,
    o_weight,
    norm_gain,
    expert_gate_up,
    expert_down,
    routes,
    route_weights,
):
    requests, steps, query_width = queries.shape
    attended = decode_attention(
        queries,
        keys_new,
        values_new,
        importance,
        merge_flags,
        key_cache,
        value_cache,
        last_weight,
        lengths,
    )
    rows = requests * steps
    width = o_weight.shape[1]
    gathered = lax.all_gather(o_weight, ("x", "c"), axis=0, tiled=True)
    lines = lax.axis_size("y")
    spread = lax.all_to_all(
        attended.reshape(rows, lines, query_width // lines),
        "y",
        split_axis=1,
        concat_axis=0,
        tiled=True,
    )
    spread = spread.reshape(lines * rows, query_width // lines)
    projected = lax.psum_scatter(
        jnp.dot(spread, gathered, preferred_element_type=jnp.float32),
        "y",
        scatter_dimension=0,
        tiled=True,
    )
    members = lax.axis_size("y") * lax.axis_size("x") * lax.axis_size("c")
    mixed = residual.reshape(rows, width).astype(jnp.float32) + projected
    normed = (
        mixed * lax.rsqrt(jnp.mean(mixed * mixed, axis=1, keepdims=True) + EPS) * norm_gain
    ).astype(jnp.bfloat16)
    experts_local = expert_gate_up.shape[0]
    dp_size = lax.axis_size("dp")
    experts_all = experts_local * dp_size * members
    top_k = routes.shape[2]
    capacity = max(2, 2 * rows * top_k // experts_all)
    chosen = routes.reshape(rows * top_k)
    sequence = jnp.arange(rows * top_k, dtype=jnp.int32)
    earlier = sequence[:, None] > sequence[None, :]
    rank = jnp.sum(((chosen[:, None] == chosen[None, :]) & earlier).astype(jnp.int32), axis=1)
    target = chosen * capacity + rank
    placing = (
        jnp.arange(experts_all * capacity, dtype=jnp.int32)[:, None] == target[None, :]
    ).reshape(experts_all * capacity, rows, top_k)
    placing = jnp.any(placing, axis=2).astype(jnp.bfloat16)
    outgoing = jnp.dot(placing, normed, preferred_element_type=jnp.float32).astype(jnp.bfloat16)
    arrived = lax.all_to_all(
        outgoing.reshape(experts_all, capacity, width),
        ("dp", "y", "x", "c"),
        split_axis=0,
        concat_axis=0,
        tiled=True,
    )
    depth = arrived.shape[1]
    sources = arrived.shape[0] // experts_local
    answer = run_experts(
        arrived.reshape(sources, experts_local, depth, width), expert_gate_up, expert_down
    )
    returned = lax.all_to_all(
        answer.reshape(sources * experts_local, depth, width),
        ("dp", "y", "x", "c"),
        split_axis=0,
        concat_axis=0,
        tiled=True,
    )
    results = returned.reshape(experts_all * capacity, width)[target].reshape(rows, top_k, width)
    blended = jnp.sum(route_weights.reshape(rows, top_k, 1) * results.astype(jnp.float32), axis=1)
    layer_out = (mixed + blended).astype(jnp.bfloat16).reshape(requests, steps, width)
    return (attended, layer_out)


def solution(mesh):
    lines = mesh.devices.shape[1] // 8
    mesh = jax.sharding.Mesh(
        mesh.devices.reshape(mesh.devices.shape[0], lines, 4, 2), ("dp", "y", "x", "c")
    )
    return jax.shard_map(
        shards,
        mesh=mesh,
        in_specs=(
            P(("dp", "y", "x", "c"), None, None),
            P(("dp", "y", "x", "c"), None, None),
            P(("dp", "y", "x", "c"), None, None),
            P(("dp", "y", "x", "c"), None, None),
            P(("dp", "y", "x", "c"), None, None),
            P(("dp", "y", "x", "c"), None, None),
            P(("dp", "y", "x", "c"), None, None),
            P(("dp", "y", "x", "c"), None),
            P(("dp", "y", "x", "c")),
            P(("dp", "y", "x", "c"), None, None),
            P(("y", "x", "c"), None),
            P(),
            P(("dp", "y", "x", "c"), None, None),
            P(("dp", "y", "x", "c"), None, None),
            P(("dp", "y", "x", "c"), None, None),
            P(("dp", "y", "x", "c"), None, None),
        ),
        out_specs=(P(("dp", "y", "x", "c"), None, None), P(("dp", "y", "x", "c"), None, None)),
        check_vma=False,
    )
```

```python
import functools
import math

import jax
import jax.numpy as jnp
from jax import lax
from jax.experimental import pallas as pl
from jax.experimental.pallas import tpu as pltpu
from jax.sharding import PartitionSpec as P

EPS = 1e-06


def decode_attention(queries, keys_new, values_new, importance, merge_flags, key_cache,
                     value_cache, last_weight, lengths):
    requests, steps, query_width = queries.shape
    heads_kv = last_weight.shape[1]
    slots, features = key_cache.shape[1], key_cache.shape[2]
    head_dim = features // heads_kv
    group = query_width // head_dim // heads_kv
    scale = 1.0 / math.sqrt(head_dim)
    f32, bf16 = jnp.float32, jnp.bfloat16

    chunk = math.gcd(slots, 128)
    window = 16

    def kernel(len_ref, flag_ref, share_ref, weight_ref, q_ref, kn_ref, vn_ref, k_ref, v_ref, o_ref):
        r = pl.program_id(0)
        n = len_ref[r]
        start = pl.multiple_of(((n - 1) // window) * window, window)
        here = lax.broadcasted_iota(jnp.int32, (window, features), 0) == (n - 1 - start)
        last_k = jnp.sum(
            jnp.where(here, k_ref[0, pl.ds(start, window), :].astype(f32), 0.0), axis=0, keepdims=True
        )
        last_v = jnp.sum(
            jnp.where(here, v_ref[0, pl.ds(start, window), :].astype(f32), 0.0), axis=0, keepdims=True
        )
        new_k = kn_ref[0].astype(f32)
        new_v = vn_ref[0].astype(f32)

        def lane_mask(flag):
            return jnp.full((1, head_dim), flag, jnp.int32) == 1

        def row_mask(flag):
            return jnp.full((group, 1), flag, jnp.int32) == 1

        tails_of = []
        for g in range(heads_kv):
            lanes = slice(g * head_dim, (g + 1) * head_dim)
            z = weight_ref[r * heads_kv + g]
            f0 = flag_ref[(r * steps) * heads_kv + g]
            f1 = flag_ref[(r * steps + 1) * heads_kv + g]
            w0 = share_ref[(r * steps) * heads_kv + g]
            w1 = share_ref[(r * steps + 1) * heads_kv + g]
            z1 = jnp.where(f0 == 1, z + w0, w0)
            m0, m1 = lane_mask(f0), lane_mask(f1)
            both = lane_mask(f0 * f1)

            def settle(last, new):
                old0 = last[:, lanes]
                n0, n1 = new[0:1, lanes], new[1:2, lanes]
                b0 = ((z * old0 + w0 * n0) / (z + w0)).astype(bf16).astype(f32)
                a0 = jnp.where(m0, b0, old0)
                cur = jnp.where(m0, a0, n0)
                b1 = ((z1 * cur + w1 * n1) / (z1 + w1)).astype(bf16).astype(f32)
                second = (
                    jnp.where(both, b1, jnp.where(m0, a0, old0)),
                    jnp.where(m0, n1, jnp.where(m1, b1, n0)),
                    n1,
                )
                return (a0, n0), second

            count0 = 2 - f0
            tails_of.append((settle(last_k, new_k), settle(last_v, new_v), (count0, count0 + 1 - f1)))

        def attend(span):
            valid = lax.broadcasted_iota(jnp.int32, (steps * group, span), 1) < n - 1
            for g in range(heads_kv):
                lanes = slice(g * head_dim, (g + 1) * head_dim)
                keys_t, values_t, counts = tails_of[g]
                rows = slice(g * group, (g + 1) * group)
                q = jnp.concatenate([q_ref[0, t, rows, :] for t in range(steps)], axis=0)
                main = (
                    lax.dot_general(
                        q, k_ref[0, 0:span, lanes], (((1,), (1,)), ((), ())),
                        preferred_element_type=f32,
                    )
                    * scale
                )
                main = jnp.where(valid, main, -jnp.inf)
                qf = q.astype(f32)
                top = jnp.max(main, axis=1, keepdims=True)
                tops, tails = [], []
                for t in range(steps):
                    here_rows = slice(t * group, (t + 1) * group)
                    top_t = top[here_rows]
                    step_tails = []
                    for j, (tk, tv) in enumerate(zip(keys_t[t], values_t[t])):
                        ts = jnp.sum(qf[here_rows] * tk, axis=1, keepdims=True) * scale
                        ts = jnp.where(row_mask((j < counts[t]).astype(jnp.int32)), ts, -jnp.inf)
                        top_t = jnp.maximum(top_t, ts)
                        step_tails.append((ts, tv))
                    tops.append(top_t)
                    tails.append(step_tails)
                top = jnp.concatenate(tops, axis=0)
                raw = jnp.exp(main - top)
                total = jnp.sum(raw, axis=1, keepdims=True)
                summed = jnp.dot(
                    raw.astype(bf16), v_ref[0, 0:span, lanes], preferred_element_type=f32
                )
                for t in range(steps):
                    here_rows = slice(t * group, (t + 1) * group)
                    total_t = total[here_rows]
                    summed_t = summed[here_rows]
                    for ts, tv in tails[t]:
                        part = jnp.exp(ts - tops[t])
                        total_t = total_t + part
                        summed_t = summed_t + part.astype(bf16).astype(f32) * tv
                    o_ref[0, t, rows, :] = (summed_t / total_t).astype(bf16)

        used = (n - 1 + chunk - 1) // chunk
        for k in range(1, slots // chunk + 1):
            pl.when(used == k)(functools.partial(attend, k * chunk))

    heads = query_width // head_dim
    per_query = pl.BlockSpec((1, steps, heads, head_dim), lambda r, *_: (r, 0, 0, 0))
    per_new = pl.BlockSpec((1, steps, features), lambda r, *_: (r, 0, 0))
    per_cache = pl.BlockSpec((1, slots, features), lambda r, *_: (r, 0, 0))
    out = pl.pallas_call(
        kernel,
        out_shape=jax.ShapeDtypeStruct((requests, steps, heads, head_dim), bf16),
        grid_spec=pltpu.PrefetchScalarGridSpec(
            num_scalar_prefetch=4,
            grid=(requests,),
            in_specs=[per_query, per_new, per_new, per_cache, per_cache],
            out_specs=per_query,
        ),
    )(
        lengths,
        merge_flags.reshape(-1),
        importance.reshape(-1),
        last_weight.reshape(-1),
        queries.reshape(requests, steps, heads, head_dim),
        keys_new,
        values_new,
        key_cache,
        value_cache,
    )
    return out.reshape(requests, steps, query_width)


def run_experts(arriving, expert_gate_up, expert_down):
    hidden_units = expert_down.shape[1]
    both = jnp.einsum(
        "sjcd,jdf->sjcf", arriving, expert_gate_up, preferred_element_type=jnp.float32
    )
    active = (jax.nn.silu(both[..., :hidden_units]) * both[..., hidden_units:]).astype(jnp.bfloat16)
    return jnp.einsum(
        "sjcf,jfd->sjcd", active, expert_down, preferred_element_type=jnp.float32
    ).astype(jnp.bfloat16)


def shards(
    queries,
    keys_new,
    values_new,
    importance,
    merge_flags,
    key_cache,
    value_cache,
    last_weight,
    lengths,
    residual,
    o_weight,
    norm_gain,
    expert_gate_up,
    expert_down,
    routes,
    route_weights,
):
    requests, steps, query_width = queries.shape
    attended = decode_attention(
        queries,
        keys_new,
        values_new,
        importance,
        merge_flags,
        key_cache,
        value_cache,
        last_weight,
        lengths,
    )
    rows = requests * steps
    width = o_weight.shape[1]
    gathered = lax.all_gather(o_weight, ("x", "c"), axis=0, tiled=True)
    lines = lax.axis_size("y")
    spread = lax.all_to_all(
        attended.reshape(rows, lines, query_width // lines),
        "y",
        split_axis=1,
        concat_axis=0,
        tiled=True,
    )
    spread = spread.reshape(lines * rows, query_width // lines)
    projected = lax.psum_scatter(
        jnp.dot(spread, gathered, preferred_element_type=jnp.float32),
        "y",
        scatter_dimension=0,
        tiled=True,
    )
    members = lax.axis_size("y") * lax.axis_size("x") * lax.axis_size("c")
    mixed = residual.reshape(rows, width).astype(jnp.float32) + projected
    normed = (
        mixed * lax.rsqrt(jnp.mean(mixed * mixed, axis=1, keepdims=True) + EPS) * norm_gain
    ).astype(jnp.bfloat16)
    experts_local = expert_gate_up.shape[0]
    dp_size = lax.axis_size("dp")
    experts_all = experts_local * dp_size * members
    top_k = routes.shape[2]
    capacity = max(2, 2 * rows * top_k // experts_all)
    chosen = routes.reshape(rows * top_k)
    sequence = jnp.arange(rows * top_k, dtype=jnp.int32)
    earlier = sequence[:, None] > sequence[None, :]
    rank = jnp.sum(((chosen[:, None] == chosen[None, :]) & earlier).astype(jnp.int32), axis=1)
    target = chosen * capacity + rank
    placing = (
        jnp.arange(experts_all * capacity, dtype=jnp.int32)[:, None] == target[None, :]
    ).reshape(experts_all * capacity, rows, top_k)
    placing = jnp.any(placing, axis=2).astype(jnp.bfloat16)
    outgoing = jnp.dot(placing, normed, preferred_element_type=jnp.float32).astype(jnp.bfloat16)
    arrived = lax.all_to_all(
        outgoing.reshape(experts_all, capacity, width),
        ("dp", "y", "x", "c"),
        split_axis=0,
        concat_axis=0,
        tiled=True,
    )
    depth = arrived.shape[1]
    sources = arrived.shape[0] // experts_local
    answer = run_experts(
        arrived.reshape(sources, experts_local, depth, width), expert_gate_up, expert_down
    )
    returned = lax.all_to_all(
        answer.reshape(sources * experts_local, depth, width),
        ("dp", "y", "x", "c"),
        split_axis=0,
        concat_axis=0,
        tiled=True,
    )
    results = returned.reshape(experts_all * capacity, width)[target].reshape(rows, top_k, width)
    blended = jnp.sum(route_weights.reshape(rows, top_k, 1) * results.astype(jnp.float32), axis=1)
    layer_out = (mixed + blended).astype(jnp.bfloat16).reshape(requests, steps, width)
    return (attended, layer_out)


def solution(mesh):
    lines = mesh.devices.shape[1] // 8
    mesh = jax.sharding.Mesh(
        mesh.devices.reshape(mesh.devices.shape[0], lines, 4, 2), ("dp", "y", "x", "c")
    )
    return jax.shard_map(
        shards,
        mesh=mesh,
        in_specs=(
            P(("dp", "y", "x", "c"), None, None),
            P(("dp", "y", "x", "c"), None, None),
            P(("dp", "y", "x", "c"), None, None),
            P(("dp", "y", "x", "c"), None, None),
            P(("dp", "y", "x", "c"), None, None),
            P(("dp", "y", "x", "c"), None, None),
            P(("dp", "y", "x", "c"), None, None),
            P(("dp", "y", "x", "c"), None),
            P(("dp", "y", "x", "c")),
            P(("dp", "y", "x", "c"), None, None),
            P(("y", "x", "c"), None),
            P(),
            P(("dp", "y", "x", "c"), None, None),
            P(("dp", "y", "x", "c"), None, None),
            P(("dp", "y", "x", "c"), None, None),
            P(("dp", "y", "x", "c"), None, None),
        ),
        out_specs=(P(("dp", "y", "x", "c"), None, None), P(("dp", "y", "x", "c"), None, None)),
        check_vma=False,
    )
```

```python
import functools
import math

import jax
import jax.numpy as jnp
from jax import lax
from jax.experimental import pallas as pl
from jax.experimental.pallas import tpu as pltpu
from jax.sharding import PartitionSpec as P

EPS = 1e-06


def decode_attention(queries, keys_new, values_new, importance, merge_flags, key_cache,
                     value_cache, last_weight, lengths):
    requests, steps, query_width = queries.shape
    heads_kv = last_weight.shape[1]
    slots, features = key_cache.shape[1], key_cache.shape[2]
    head_dim = features // heads_kv
    group = query_width // head_dim // heads_kv
    scale = 1.0 / math.sqrt(head_dim)
    f32, bf16 = jnp.float32, jnp.bfloat16

    chunk = math.gcd(slots, 128)
    window = 16

    chunks = slots // chunk

    def kernel(len_ref, flag_ref, share_ref, weight_ref, q_ref, kn_ref, vn_ref, k_hbm, v_hbm, o_ref,
               k_buf, v_buf, sems):
        r = pl.program_id(0)
        n = len_ref[r]
        here_buf = r % 2

        def copies(req, buf):
            needed = (len_ref[req] - 1) // chunk + 1
            for c in range(chunks):
                part = pl.ds(c * chunk, chunk)
                for a, (src, dst) in enumerate(((k_hbm, k_buf), (v_hbm, v_buf))):
                    copy = pltpu.make_async_copy(
                        src.at[req, part], dst.at[buf, part], sems.at[a, buf, c]
                    )
                    yield c < needed, copy

        def start_all(req, buf):
            for cond, copy in copies(req, buf):
                pl.when(cond)(copy.start)

        @pl.when(r == 0)
        def _():
            start_all(0, 0)

        @pl.when(r + 1 < requests)
        def _():
            start_all(r + 1, 1 - here_buf)

        for cond, copy in copies(r, here_buf):
            pl.when(cond)(copy.wait)
        k_ref = k_buf.at[here_buf]
        v_ref = v_buf.at[here_buf]
        start = pl.multiple_of(((n - 1) // window) * window, window)
        here = lax.broadcasted_iota(jnp.int32, (window, features), 0) == (n - 1 - start)
        last_k = jnp.sum(
            jnp.where(here, k_ref[pl.ds(start, window), :].astype(f32), 0.0), axis=0, keepdims=True
        )
        last_v = jnp.sum(
            jnp.where(here, v_ref[pl.ds(start, window), :].astype(f32), 0.0), axis=0, keepdims=True
        )
        new_k = kn_ref[0].astype(f32)
        new_v = vn_ref[0].astype(f32)

        def lane_mask(flag):
            return jnp.full((1, head_dim), flag, jnp.int32) == 1

        def row_mask(flag):
            return jnp.full((group, 1), flag, jnp.int32) == 1

        tails_of = []
        for g in range(heads_kv):
            lanes = slice(g * head_dim, (g + 1) * head_dim)
            z = weight_ref[r * heads_kv + g]
            f0 = flag_ref[(r * steps) * heads_kv + g]
            f1 = flag_ref[(r * steps + 1) * heads_kv + g]
            w0 = share_ref[(r * steps) * heads_kv + g]
            w1 = share_ref[(r * steps + 1) * heads_kv + g]
            z1 = jnp.where(f0 == 1, z + w0, w0)
            m0, m1 = lane_mask(f0), lane_mask(f1)
            both = lane_mask(f0 * f1)

            def settle(last, new):
                old0 = last[:, lanes]
                n0, n1 = new[0:1, lanes], new[1:2, lanes]
                b0 = ((z * old0 + w0 * n0) / (z + w0)).astype(bf16).astype(f32)
                a0 = jnp.where(m0, b0, old0)
                cur = jnp.where(m0, a0, n0)
                b1 = ((z1 * cur + w1 * n1) / (z1 + w1)).astype(bf16).astype(f32)
                second = (
                    jnp.where(both, b1, jnp.where(m0, a0, old0)),
                    jnp.where(m0, n1, jnp.where(m1, b1, n0)),
                    n1,
                )
                return (a0, n0), second

            count0 = 2 - f0
            tails_of.append((settle(last_k, new_k), settle(last_v, new_v), (count0, count0 + 1 - f1)))

        def attend(span):
            valid = lax.broadcasted_iota(jnp.int32, (steps * group, span), 1) < n - 1
            for g in range(heads_kv):
                lanes = slice(g * head_dim, (g + 1) * head_dim)
                keys_t, values_t, counts = tails_of[g]
                rows = slice(g * group, (g + 1) * group)
                q = jnp.concatenate([q_ref[0, t, rows, :] for t in range(steps)], axis=0)
                main = (
                    lax.dot_general(
                        q, k_ref[0:span, lanes], (((1,), (1,)), ((), ())),
                        preferred_element_type=f32,
                    )
                    * scale
                )
                main = jnp.where(valid, main, -jnp.inf)
                qf = q.astype(f32)
                top = jnp.max(main, axis=1, keepdims=True)
                tops, tails = [], []
                for t in range(steps):
                    here_rows = slice(t * group, (t + 1) * group)
                    top_t = top[here_rows]
                    step_tails = []
                    for j, (tk, tv) in enumerate(zip(keys_t[t], values_t[t])):
                        ts = jnp.sum(qf[here_rows] * tk, axis=1, keepdims=True) * scale
                        ts = jnp.where(row_mask((j < counts[t]).astype(jnp.int32)), ts, -jnp.inf)
                        top_t = jnp.maximum(top_t, ts)
                        step_tails.append((ts, tv))
                    tops.append(top_t)
                    tails.append(step_tails)
                top = jnp.concatenate(tops, axis=0)
                raw = jnp.exp(main - top)
                total = jnp.sum(raw, axis=1, keepdims=True)
                summed = jnp.dot(
                    raw.astype(bf16), v_ref[0:span, lanes], preferred_element_type=f32
                )
                for t in range(steps):
                    here_rows = slice(t * group, (t + 1) * group)
                    total_t = total[here_rows]
                    summed_t = summed[here_rows]
                    for ts, tv in tails[t]:
                        part = jnp.exp(ts - tops[t])
                        total_t = total_t + part
                        summed_t = summed_t + part.astype(bf16).astype(f32) * tv
                    o_ref[0, t, rows, :] = (summed_t / total_t).astype(bf16)

        used = (n - 1) // chunk + 1
        for k in range(1, slots // chunk + 1):
            pl.when(used == k)(functools.partial(attend, k * chunk))

    heads = query_width // head_dim
    per_query = pl.BlockSpec((1, steps, heads, head_dim), lambda r, *_: (r, 0, 0, 0))
    per_new = pl.BlockSpec((1, steps, features), lambda r, *_: (r, 0, 0))
    per_cache = pl.BlockSpec(memory_space=pl.ANY)
    out = pl.pallas_call(
        kernel,
        out_shape=jax.ShapeDtypeStruct((requests, steps, heads, head_dim), bf16),
        grid_spec=pltpu.PrefetchScalarGridSpec(
            num_scalar_prefetch=4,
            grid=(requests,),
            in_specs=[per_query, per_new, per_new, per_cache, per_cache],
            out_specs=per_query,
            scratch_shapes=[
                pltpu.VMEM((2, slots, features), key_cache.dtype),
                pltpu.VMEM((2, slots, features), value_cache.dtype),
                pltpu.SemaphoreType.DMA((2, 2, chunks)),
            ],
        ),
    )(
        lengths,
        merge_flags.reshape(-1),
        importance.reshape(-1),
        last_weight.reshape(-1),
        queries.reshape(requests, steps, heads, head_dim),
        keys_new,
        values_new,
        key_cache,
        value_cache,
    )
    return out.reshape(requests, steps, query_width)


def run_experts(arriving, expert_gate_up, expert_down):
    hidden_units = expert_down.shape[1]
    both = jnp.einsum(
        "sjcd,jdf->sjcf", arriving, expert_gate_up, preferred_element_type=jnp.float32
    )
    active = (jax.nn.silu(both[..., :hidden_units]) * both[..., hidden_units:]).astype(jnp.bfloat16)
    return jnp.einsum(
        "sjcf,jfd->sjcd", active, expert_down, preferred_element_type=jnp.float32
    ).astype(jnp.bfloat16)


def shards(
    queries,
    keys_new,
    values_new,
    importance,
    merge_flags,
    key_cache,
    value_cache,
    last_weight,
    lengths,
    residual,
    o_weight,
    norm_gain,
    expert_gate_up,
    expert_down,
    routes,
    route_weights,
):
    requests, steps, query_width = queries.shape
    attended = decode_attention(
        queries,
        keys_new,
        values_new,
        importance,
        merge_flags,
        key_cache,
        value_cache,
        last_weight,
        lengths,
    )
    rows = requests * steps
    width = o_weight.shape[1]
    gathered = lax.all_gather(o_weight, ("x", "c"), axis=0, tiled=True)
    lines = lax.axis_size("y")
    spread = lax.all_to_all(
        attended.reshape(rows, lines, query_width // lines),
        "y",
        split_axis=1,
        concat_axis=0,
        tiled=True,
    )
    spread = spread.reshape(lines * rows, query_width // lines)
    projected = lax.psum_scatter(
        jnp.dot(spread, gathered, preferred_element_type=jnp.float32),
        "y",
        scatter_dimension=0,
        tiled=True,
    )
    members = lax.axis_size("y") * lax.axis_size("x") * lax.axis_size("c")
    mixed = residual.reshape(rows, width).astype(jnp.float32) + projected
    normed = (
        mixed * lax.rsqrt(jnp.mean(mixed * mixed, axis=1, keepdims=True) + EPS) * norm_gain
    ).astype(jnp.bfloat16)
    experts_local = expert_gate_up.shape[0]
    dp_size = lax.axis_size("dp")
    experts_all = experts_local * dp_size * members
    top_k = routes.shape[2]
    capacity = max(2, 2 * rows * top_k // experts_all)
    chosen = routes.reshape(rows * top_k)
    sequence = jnp.arange(rows * top_k, dtype=jnp.int32)
    earlier = sequence[:, None] > sequence[None, :]
    rank = jnp.sum(((chosen[:, None] == chosen[None, :]) & earlier).astype(jnp.int32), axis=1)
    target = chosen * capacity + rank
    placing = (
        jnp.arange(experts_all * capacity, dtype=jnp.int32)[:, None] == target[None, :]
    ).reshape(experts_all * capacity, rows, top_k)
    placing = jnp.any(placing, axis=2).astype(jnp.bfloat16)
    outgoing = jnp.dot(placing, normed, preferred_element_type=jnp.float32).astype(jnp.bfloat16)
    arrived = lax.all_to_all(
        outgoing.reshape(experts_all, capacity, width),
        ("dp", "y", "x", "c"),
        split_axis=0,
        concat_axis=0,
        tiled=True,
    )
    depth = arrived.shape[1]
    sources = arrived.shape[0] // experts_local
    answer = run_experts(
        arrived.reshape(sources, experts_local, depth, width), expert_gate_up, expert_down
    )
    returned = lax.all_to_all(
        answer.reshape(sources * experts_local, depth, width),
        ("dp", "y", "x", "c"),
        split_axis=0,
        concat_axis=0,
        tiled=True,
    )
    results = returned.reshape(experts_all * capacity, width)[target].reshape(rows, top_k, width)
    blended = jnp.sum(route_weights.reshape(rows, top_k, 1) * results.astype(jnp.float32), axis=1)
    layer_out = (mixed + blended).astype(jnp.bfloat16).reshape(requests, steps, width)
    return (attended, layer_out)


def solution(mesh):
    lines = mesh.devices.shape[1] // 8
    mesh = jax.sharding.Mesh(
        mesh.devices.reshape(mesh.devices.shape[0], lines, 4, 2), ("dp", "y", "x", "c")
    )
    return jax.shard_map(
        shards,
        mesh=mesh,
        in_specs=(
            P(("dp", "y", "x", "c"), None, None),
            P(("dp", "y", "x", "c"), None, None),
            P(("dp", "y", "x", "c"), None, None),
            P(("dp", "y", "x", "c"), None, None),
            P(("dp", "y", "x", "c"), None, None),
            P(("dp", "y", "x", "c"), None, None),
            P(("dp", "y", "x", "c"), None, None),
            P(("dp", "y", "x", "c"), None),
            P(("dp", "y", "x", "c")),
            P(("dp", "y", "x", "c"), None, None),
            P(("y", "x", "c"), None),
            P(),
            P(("dp", "y", "x", "c"), None, None),
            P(("dp", "y", "x", "c"), None, None),
            P(("dp", "y", "x", "c"), None, None),
            P(("dp", "y", "x", "c"), None, None),
        ),
        out_specs=(P(("dp", "y", "x", "c"), None, None), P(("dp", "y", "x", "c"), None, None)),
        check_vma=False,
    )
```

```python
import functools
import math

import jax
import jax.numpy as jnp
from jax import lax
from jax.experimental import pallas as pl
from jax.experimental.pallas import tpu as pltpu
from jax.sharding import PartitionSpec as P

EPS = 1e-06


def decode_attention(queries, keys_new, values_new, importance, merge_flags, key_cache,
                     value_cache, last_weight, lengths):
    requests, steps, query_width = queries.shape
    heads_kv = last_weight.shape[1]
    slots, features = key_cache.shape[1], key_cache.shape[2]
    head_dim = features // heads_kv
    group = query_width // head_dim // heads_kv
    scale = 1.0 / math.sqrt(head_dim)
    f32, bf16 = jnp.float32, jnp.bfloat16

    chunk = math.gcd(slots, 128)
    window = 16

    chunks = slots // chunk

    def kernel(len_ref, flag_ref, share_ref, weight_ref, q_ref, kn_ref, vn_ref, k_hbm, v_hbm, o_ref,
               k_buf, v_buf, sems):
        r = pl.program_id(0)
        n = len_ref[r]
        here_buf = r % 2

        def copies(req, buf):
            needed = (len_ref[req] - 1) // chunk + 1
            for c in range(chunks):
                part = pl.ds(c * chunk, chunk)
                for a, (src, dst) in enumerate(((k_hbm, k_buf), (v_hbm, v_buf))):
                    copy = pltpu.make_async_copy(
                        src.at[req, part], dst.at[buf, part], sems.at[a, buf, c]
                    )
                    yield c < needed, copy

        def start_all(req, buf):
            for cond, copy in copies(req, buf):
                pl.when(cond)(copy.start)

        @pl.when(r == 0)
        def _():
            start_all(0, 0)

        @pl.when(r + 1 < requests)
        def _():
            start_all(r + 1, 1 - here_buf)

        for cond, copy in copies(r, here_buf):
            pl.when(cond)(copy.wait)
        k_ref = k_buf.at[here_buf]
        v_ref = v_buf.at[here_buf]
        start = pl.multiple_of(((n - 1) // window) * window, window)
        here = lax.broadcasted_iota(jnp.int32, (window, features), 0) == (n - 1 - start)
        last_k = jnp.sum(
            jnp.where(here, k_ref[pl.ds(start, window), :].astype(f32), 0.0), axis=0, keepdims=True
        )
        last_v = jnp.sum(
            jnp.where(here, v_ref[pl.ds(start, window), :].astype(f32), 0.0), axis=0, keepdims=True
        )
        new_k = kn_ref[0].astype(f32)
        new_v = vn_ref[0].astype(f32)

        def lane_mask(flag):
            return jnp.full((1, head_dim), flag, jnp.int32) == 1

        def row_mask(flag):
            return jnp.full((group, 1), flag, jnp.int32) == 1

        tails_of = []
        for g in range(heads_kv):
            lanes = slice(g * head_dim, (g + 1) * head_dim)
            z = weight_ref[r * heads_kv + g]
            f0 = flag_ref[(r * steps) * heads_kv + g]
            f1 = flag_ref[(r * steps + 1) * heads_kv + g]
            w0 = share_ref[(r * steps) * heads_kv + g]
            w1 = share_ref[(r * steps + 1) * heads_kv + g]
            z1 = jnp.where(f0 == 1, z + w0, w0)
            m0, m1 = lane_mask(f0), lane_mask(f1)
            both = lane_mask(f0 * f1)

            def settle(last, new):
                old0 = last[:, lanes]
                n0, n1 = new[0:1, lanes], new[1:2, lanes]
                b0 = ((z * old0 + w0 * n0) / (z + w0)).astype(bf16).astype(f32)
                a0 = jnp.where(m0, b0, old0)
                cur = jnp.where(m0, a0, n0)
                b1 = ((z1 * cur + w1 * n1) / (z1 + w1)).astype(bf16).astype(f32)
                second = (
                    jnp.where(both, b1, jnp.where(m0, a0, old0)),
                    jnp.where(m0, n1, jnp.where(m1, b1, n0)),
                    n1,
                )
                return (a0, n0), second

            count0 = 2 - f0
            tails_of.append((settle(last_k, new_k), settle(last_v, new_v), (count0, count0 + 1 - f1)))

        def attend(span):
            valid = lax.broadcasted_iota(jnp.int32, (steps * group, span), 1) < n - 1
            for g in range(heads_kv):
                lanes = slice(g * head_dim, (g + 1) * head_dim)
                keys_t, values_t, counts = tails_of[g]
                rows = slice(g * group, (g + 1) * group)
                q = jnp.concatenate([q_ref[0, t, rows, :] for t in range(steps)], axis=0)
                main = (
                    lax.dot_general(
                        q, k_ref[0:span, lanes], (((1,), (1,)), ((), ())),
                        preferred_element_type=f32,
                    )
                    * scale
                )
                main = jnp.where(valid, main, -jnp.inf)
                qf = q.astype(f32)
                top = jnp.max(main, axis=1, keepdims=True)
                tops, tails = [], []
                for t in range(steps):
                    here_rows = slice(t * group, (t + 1) * group)
                    top_t = top[here_rows]
                    step_tails = []
                    for j, (tk, tv) in enumerate(zip(keys_t[t], values_t[t])):
                        ts = jnp.sum(qf[here_rows] * tk, axis=1, keepdims=True) * scale
                        ts = jnp.where(row_mask((j < counts[t]).astype(jnp.int32)), ts, -jnp.inf)
                        top_t = jnp.maximum(top_t, ts)
                        step_tails.append((ts, tv))
                    tops.append(top_t)
                    tails.append(step_tails)
                top = jnp.concatenate(tops, axis=0)
                raw = jnp.exp(main - top)
                total = jnp.sum(raw, axis=1, keepdims=True)
                summed = jnp.dot(
                    raw.astype(bf16), v_ref[0:span, lanes], preferred_element_type=f32
                )
                for t in range(steps):
                    here_rows = slice(t * group, (t + 1) * group)
                    total_t = total[here_rows]
                    summed_t = summed[here_rows]
                    for ts, tv in tails[t]:
                        part = jnp.exp(ts - tops[t])
                        total_t = total_t + part
                        summed_t = summed_t + part.astype(bf16).astype(f32) * tv
                    o_ref[0, t, rows, :] = (summed_t / total_t).astype(bf16)

        used = (n - 1) // chunk + 1
        for k in range(1, slots // chunk + 1):
            pl.when(used == k)(functools.partial(attend, k * chunk))

    heads = query_width // head_dim
    per_query = pl.BlockSpec((1, steps, heads, head_dim), lambda r, *_: (r, 0, 0, 0))
    per_new = pl.BlockSpec((1, steps, features), lambda r, *_: (r, 0, 0))
    per_cache = pl.BlockSpec(memory_space=pl.ANY)
    out = pl.pallas_call(
        kernel,
        out_shape=jax.ShapeDtypeStruct((requests, steps, heads, head_dim), bf16),
        grid_spec=pltpu.PrefetchScalarGridSpec(
            num_scalar_prefetch=4,
            grid=(requests,),
            in_specs=[per_query, per_new, per_new, per_cache, per_cache],
            out_specs=per_query,
            scratch_shapes=[
                pltpu.VMEM((2, slots, features), key_cache.dtype),
                pltpu.VMEM((2, slots, features), value_cache.dtype),
                pltpu.SemaphoreType.DMA((2, 2, chunks)),
            ],
        ),
    )(
        lengths,
        merge_flags.reshape(-1),
        importance.reshape(-1),
        last_weight.reshape(-1),
        queries.reshape(requests, steps, heads, head_dim),
        keys_new,
        values_new,
        key_cache,
        value_cache,
    )
    return out.reshape(requests, steps, query_width)


def run_experts(arriving, expert_gate_up, expert_down):
    hidden_units = expert_down.shape[1]
    both = jnp.einsum(
        "sjcd,jdf->sjcf", arriving, expert_gate_up, preferred_element_type=jnp.float32
    )
    active = (jax.nn.silu(both[..., :hidden_units]) * both[..., hidden_units:]).astype(jnp.bfloat16)
    return jnp.einsum(
        "sjcf,jfd->sjcd", active, expert_down, preferred_element_type=jnp.float32
    ).astype(jnp.bfloat16)


def shards(
    queries,
    keys_new,
    values_new,
    importance,
    merge_flags,
    key_cache,
    value_cache,
    last_weight,
    lengths,
    residual,
    o_weight,
    norm_gain,
    expert_gate_up,
    expert_down,
    routes,
    route_weights,
):
    requests, steps, query_width = queries.shape
    attended = decode_attention(
        queries,
        keys_new,
        values_new,
        importance,
        merge_flags,
        key_cache,
        value_cache,
        last_weight,
        lengths,
    )
    rows = requests * steps
    width = o_weight.shape[1]
    gathered = lax.all_gather(o_weight, ("x", "c"), axis=0, tiled=True)
    lines = lax.axis_size("y")
    spread = lax.all_to_all(
        attended.reshape(rows, lines, query_width // lines),
        "y",
        split_axis=1,
        concat_axis=0,
        tiled=True,
    )
    spread = spread.reshape(lines * rows, query_width // lines)
    projected = lax.psum_scatter(
        jnp.dot(spread, gathered, preferred_element_type=jnp.float32).astype(jnp.bfloat16),
        "y",
        scatter_dimension=0,
        tiled=True,
    )
    members = lax.axis_size("y") * lax.axis_size("x") * lax.axis_size("c")
    mixed = residual.reshape(rows, width).astype(jnp.float32) + projected.astype(jnp.float32)
    normed = (
        mixed * lax.rsqrt(jnp.mean(mixed * mixed, axis=1, keepdims=True) + EPS) * norm_gain
    ).astype(jnp.bfloat16)
    experts_local = expert_gate_up.shape[0]
    dp_size = lax.axis_size("dp")
    experts_all = experts_local * dp_size * members
    top_k = routes.shape[2]
    capacity = max(2, 2 * rows * top_k // experts_all)
    chosen = routes.reshape(rows * top_k)
    sequence = jnp.arange(rows * top_k, dtype=jnp.int32)
    earlier = sequence[:, None] > sequence[None, :]
    rank = jnp.sum(((chosen[:, None] == chosen[None, :]) & earlier).astype(jnp.int32), axis=1)
    target = chosen * capacity + rank
    placing = (
        jnp.arange(experts_all * capacity, dtype=jnp.int32)[:, None] == target[None, :]
    ).reshape(experts_all * capacity, rows, top_k)
    placing = jnp.any(placing, axis=2).astype(jnp.bfloat16)
    outgoing = jnp.dot(placing, normed, preferred_element_type=jnp.float32).astype(jnp.bfloat16)
    arrived = lax.all_to_all(
        outgoing.reshape(experts_all, capacity, width),
        ("dp", "y", "x", "c"),
        split_axis=0,
        concat_axis=0,
        tiled=True,
    )
    depth = arrived.shape[1]
    sources = arrived.shape[0] // experts_local
    answer = run_experts(
        arrived.reshape(sources, experts_local, depth, width), expert_gate_up, expert_down
    )
    returned = lax.all_to_all(
        answer.reshape(sources * experts_local, depth, width),
        ("dp", "y", "x", "c"),
        split_axis=0,
        concat_axis=0,
        tiled=True,
    )
    slots_all = jnp.arange(experts_all * capacity, dtype=jnp.int32)
    gathering = jnp.sum(
        jnp.where(
            slots_all[None, None, :] == target.reshape(rows, top_k, 1),
            route_weights.reshape(rows, top_k, 1),
            0.0,
        ),
        axis=1,
    )
    blended = jnp.dot(
        gathering,
        returned.reshape(experts_all * capacity, width).astype(jnp.float32),
        precision=lax.Precision.HIGHEST,
        preferred_element_type=jnp.float32,
    )
    layer_out = (mixed + blended).astype(jnp.bfloat16).reshape(requests, steps, width)
    return (attended, layer_out)


def solution(mesh):
    lines = mesh.devices.shape[1] // 8
    mesh = jax.sharding.Mesh(
        mesh.devices.reshape(mesh.devices.shape[0], lines, 4, 2), ("dp", "y", "x", "c")
    )
    return jax.shard_map(
        shards,
        mesh=mesh,
        in_specs=(
            P(("dp", "y", "x", "c"), None, None),
            P(("dp", "y", "x", "c"), None, None),
            P(("dp", "y", "x", "c"), None, None),
            P(("dp", "y", "x", "c"), None, None),
            P(("dp", "y", "x", "c"), None, None),
            P(("dp", "y", "x", "c"), None, None),
            P(("dp", "y", "x", "c"), None, None),
            P(("dp", "y", "x", "c"), None),
            P(("dp", "y", "x", "c")),
            P(("dp", "y", "x", "c"), None, None),
            P(("y", "x", "c"), None),
            P(),
            P(("dp", "y", "x", "c"), None, None),
            P(("dp", "y", "x", "c"), None, None),
            P(("dp", "y", "x", "c"), None, None),
            P(("dp", "y", "x", "c"), None, None),
        ),
        out_specs=(P(("dp", "y", "x", "c"), None, None), P(("dp", "y", "x", "c"), None, None)),
        check_vma=False,
    )
```

```python
import functools
import math

import jax
import jax.numpy as jnp
from jax import lax
from jax.experimental import pallas as pl
from jax.experimental.pallas import tpu as pltpu
from jax.sharding import PartitionSpec as P

EPS = 1e-06


def decode_attention(queries, keys_new, values_new, importance, merge_flags, key_cache,
                     value_cache, last_weight, lengths):
    requests, steps, query_width = queries.shape
    heads_kv = last_weight.shape[1]
    slots, features = key_cache.shape[1], key_cache.shape[2]
    head_dim = features // heads_kv
    group = query_width // head_dim // heads_kv
    scale = 1.0 / math.sqrt(head_dim)
    f32, bf16 = jnp.float32, jnp.bfloat16

    chunk = math.gcd(slots, 128)
    window = 16

    chunks = slots // chunk

    def kernel(len_ref, flag_ref, share_ref, weight_ref, q_ref, kn_ref, vn_ref, k_hbm, v_hbm, o_ref,
               k_buf, v_buf, sems):
        r = pl.program_id(0)
        n = len_ref[r]
        here_buf = r % 2

        def copies(req, buf):
            needed = (len_ref[req] - 1) // chunk + 1
            for c in range(chunks):
                part = pl.ds(c * chunk, chunk)
                for a, (src, dst) in enumerate(((k_hbm, k_buf), (v_hbm, v_buf))):
                    copy = pltpu.make_async_copy(
                        src.at[req, part], dst.at[buf, part], sems.at[a, buf, c]
                    )
                    yield c < needed, copy

        def start_all(req, buf):
            for cond, copy in copies(req, buf):
                pl.when(cond)(copy.start)

        @pl.when(r == 0)
        def _():
            start_all(0, 0)

        @pl.when(r + 1 < requests)
        def _():
            start_all(r + 1, 1 - here_buf)

        for cond, copy in copies(r, here_buf):
            pl.when(cond)(copy.wait)
        k_ref = k_buf.at[here_buf]
        v_ref = v_buf.at[here_buf]
        start = pl.multiple_of(((n - 1) // window) * window, window)
        here = lax.broadcasted_iota(jnp.int32, (window, features), 0) == (n - 1 - start)
        last_k = jnp.sum(
            jnp.where(here, k_ref[pl.ds(start, window), :].astype(f32), 0.0), axis=0, keepdims=True
        )
        last_v = jnp.sum(
            jnp.where(here, v_ref[pl.ds(start, window), :].astype(f32), 0.0), axis=0, keepdims=True
        )
        new_k = kn_ref[0].astype(f32)
        new_v = vn_ref[0].astype(f32)

        def lane_mask(flag):
            return jnp.full((1, head_dim), flag, jnp.int32) == 1

        def row_mask(flag):
            return jnp.full((group, 1), flag, jnp.int32) == 1

        tails_of = []
        for g in range(heads_kv):
            lanes = slice(g * head_dim, (g + 1) * head_dim)
            z = weight_ref[r * heads_kv + g]
            f0 = flag_ref[(r * steps) * heads_kv + g]
            f1 = flag_ref[(r * steps + 1) * heads_kv + g]
            w0 = share_ref[(r * steps) * heads_kv + g]
            w1 = share_ref[(r * steps + 1) * heads_kv + g]
            z1 = jnp.where(f0 == 1, z + w0, w0)
            m0, m1 = lane_mask(f0), lane_mask(f1)
            both = lane_mask(f0 * f1)

            def settle(last, new):
                old0 = last[:, lanes]
                n0, n1 = new[0:1, lanes], new[1:2, lanes]
                b0 = ((z * old0 + w0 * n0) / (z + w0)).astype(bf16).astype(f32)
                a0 = jnp.where(m0, b0, old0)
                cur = jnp.where(m0, a0, n0)
                b1 = ((z1 * cur + w1 * n1) / (z1 + w1)).astype(bf16).astype(f32)
                second = (
                    jnp.where(both, b1, jnp.where(m0, a0, old0)),
                    jnp.where(m0, n1, jnp.where(m1, b1, n0)),
                    n1,
                )
                return (a0, n0), second

            count0 = 2 - f0
            tails_of.append((settle(last_k, new_k), settle(last_v, new_v), (count0, count0 + 1 - f1)))

        def attend(span):
            valid = lax.broadcasted_iota(jnp.int32, (steps * group, span), 1) < n - 1
            for g in range(heads_kv):
                lanes = slice(g * head_dim, (g + 1) * head_dim)
                keys_t, values_t, counts = tails_of[g]
                rows = slice(g * group, (g + 1) * group)
                q = jnp.concatenate([q_ref[0, t, rows, :] for t in range(steps)], axis=0)
                main = (
                    lax.dot_general(
                        q, k_ref[0:span, lanes], (((1,), (1,)), ((), ())),
                        preferred_element_type=f32,
                    )
                    * scale
                )
                main = jnp.where(valid, main, -jnp.inf)
                qf = q.astype(f32)
                top = jnp.max(main, axis=1, keepdims=True)
                tops, tails = [], []
                for t in range(steps):
                    here_rows = slice(t * group, (t + 1) * group)
                    top_t = top[here_rows]
                    step_tails = []
                    for j, (tk, tv) in enumerate(zip(keys_t[t], values_t[t])):
                        ts = jnp.sum(qf[here_rows] * tk, axis=1, keepdims=True) * scale
                        ts = jnp.where(row_mask((j < counts[t]).astype(jnp.int32)), ts, -jnp.inf)
                        top_t = jnp.maximum(top_t, ts)
                        step_tails.append((ts, tv))
                    tops.append(top_t)
                    tails.append(step_tails)
                top = jnp.concatenate(tops, axis=0)
                raw = jnp.exp(main - top)
                total = jnp.sum(raw, axis=1, keepdims=True)
                summed = jnp.dot(
                    raw.astype(bf16), v_ref[0:span, lanes], preferred_element_type=f32
                )
                for t in range(steps):
                    here_rows = slice(t * group, (t + 1) * group)
                    total_t = total[here_rows]
                    summed_t = summed[here_rows]
                    for ts, tv in tails[t]:
                        part = jnp.exp(ts - tops[t])
                        total_t = total_t + part
                        summed_t = summed_t + part.astype(bf16).astype(f32) * tv
                    o_ref[0, t, rows, :] = (summed_t / total_t).astype(bf16)

        used = (n - 1) // chunk + 1
        for k in range(1, slots // chunk + 1):
            pl.when(used == k)(functools.partial(attend, k * chunk))

    heads = query_width // head_dim
    per_query = pl.BlockSpec((1, steps, heads, head_dim), lambda r, *_: (r, 0, 0, 0))
    per_new = pl.BlockSpec((1, steps, features), lambda r, *_: (r, 0, 0))
    per_cache = pl.BlockSpec(memory_space=pl.ANY)
    out = pl.pallas_call(
        kernel,
        out_shape=jax.ShapeDtypeStruct((requests, steps, heads, head_dim), bf16),
        grid_spec=pltpu.PrefetchScalarGridSpec(
            num_scalar_prefetch=4,
            grid=(requests,),
            in_specs=[per_query, per_new, per_new, per_cache, per_cache],
            out_specs=per_query,
            scratch_shapes=[
                pltpu.VMEM((2, slots, features), key_cache.dtype),
                pltpu.VMEM((2, slots, features), value_cache.dtype),
                pltpu.SemaphoreType.DMA((2, 2, chunks)),
            ],
        ),
    )(
        lengths,
        merge_flags.reshape(-1),
        importance.reshape(-1),
        last_weight.reshape(-1),
        queries.reshape(requests, steps, heads, head_dim),
        keys_new,
        values_new,
        key_cache,
        value_cache,
    )
    return out.reshape(requests, steps, query_width)


def run_experts(arriving, expert_gate_up, expert_down):
    hidden_units = expert_down.shape[1]
    both = jnp.einsum(
        "sjcd,jdf->sjcf", arriving, expert_gate_up, preferred_element_type=jnp.float32
    )
    active = (jax.nn.silu(both[..., :hidden_units]) * both[..., hidden_units:]).astype(jnp.bfloat16)
    return jnp.einsum(
        "sjcf,jfd->sjcd", active, expert_down, preferred_element_type=jnp.float32
    ).astype(jnp.bfloat16)


def shards(
    queries,
    keys_new,
    values_new,
    importance,
    merge_flags,
    key_cache,
    value_cache,
    last_weight,
    lengths,
    residual,
    o_weight,
    norm_gain,
    expert_gate_up,
    expert_down,
    routes,
    route_weights,
):
    requests, steps, query_width = queries.shape
    attended = decode_attention(
        queries,
        keys_new,
        values_new,
        importance,
        merge_flags,
        key_cache,
        value_cache,
        last_weight,
        lengths,
    )
    rows = requests * steps
    width = o_weight.shape[1]
    gathered = lax.all_gather(o_weight, ("x", "c"), axis=0, tiled=True)
    lines = lax.axis_size("y")
    line = lax.axis_index("y")
    block = query_width // lines
    flat = attended.reshape(rows, query_width)

    def shifted(value, shift):
        return lax.ppermute(value, "y", [(j, (j + shift) % lines) for j in range(lines)])

    pieces = [lax.dynamic_slice_in_dim(flat, line * block, block, 1)]
    for shift in range(1, lines):
        piece = lax.dynamic_slice_in_dim(flat, ((line + shift) % lines) * block, block, 1)
        pieces.append(shifted(piece, shift))
    partials = jnp.dot(
        jnp.concatenate(pieces, axis=0), gathered, preferred_element_type=jnp.float32
    ).reshape(lines, rows, width)
    projected = partials[0]
    for shift in range(1, lines):
        projected = projected + shifted(partials[shift], lines - shift)
    members = lax.axis_size("y") * lax.axis_size("x") * lax.axis_size("c")
    mixed = residual.reshape(rows, width).astype(jnp.float32) + projected
    normed = (
        mixed * lax.rsqrt(jnp.mean(mixed * mixed, axis=1, keepdims=True) + EPS) * norm_gain
    ).astype(jnp.bfloat16)
    experts_local = expert_gate_up.shape[0]
    dp_size = lax.axis_size("dp")
    experts_all = experts_local * dp_size * members
    top_k = routes.shape[2]
    capacity = max(2, 2 * rows * top_k // experts_all)
    chosen = routes.reshape(rows * top_k)
    sequence = jnp.arange(rows * top_k, dtype=jnp.int32)
    earlier = sequence[:, None] > sequence[None, :]
    rank = jnp.sum(((chosen[:, None] == chosen[None, :]) & earlier).astype(jnp.int32), axis=1)
    target = chosen * capacity + rank
    placing = (
        jnp.arange(experts_all * capacity, dtype=jnp.int32)[:, None] == target[None, :]
    ).reshape(experts_all * capacity, rows, top_k)
    placing = jnp.any(placing, axis=2).astype(jnp.bfloat16)
    outgoing = jnp.dot(placing, normed, preferred_element_type=jnp.float32).astype(jnp.bfloat16)
    arrived = lax.all_to_all(
        outgoing.reshape(experts_all, capacity, width),
        ("dp", "y", "x", "c"),
        split_axis=0,
        concat_axis=0,
        tiled=True,
    )
    depth = arrived.shape[1]
    sources = arrived.shape[0] // experts_local
    answer = run_experts(
        arrived.reshape(sources, experts_local, depth, width), expert_gate_up, expert_down
    )
    returned = lax.all_to_all(
        answer.reshape(sources * experts_local, depth, width),
        ("dp", "y", "x", "c"),
        split_axis=0,
        concat_axis=0,
        tiled=True,
    )
    slots_all = jnp.arange(experts_all * capacity, dtype=jnp.int32)
    gathering = jnp.sum(
        jnp.where(
            slots_all[None, None, :] == target.reshape(rows, top_k, 1),
            route_weights.reshape(rows, top_k, 1),
            0.0,
        ),
        axis=1,
    )
    blended = jnp.dot(
        gathering,
        returned.reshape(experts_all * capacity, width).astype(jnp.float32),
        precision=lax.Precision.HIGHEST,
        preferred_element_type=jnp.float32,
    )
    layer_out = (mixed + blended).astype(jnp.bfloat16).reshape(requests, steps, width)
    return (attended, layer_out)


def solution(mesh):
    lines = mesh.devices.shape[1] // 8
    mesh = jax.sharding.Mesh(
        mesh.devices.reshape(mesh.devices.shape[0], lines, 4, 2), ("dp", "y", "x", "c")
    )
    return jax.shard_map(
        shards,
        mesh=mesh,
        in_specs=(
            P(("dp", "y", "x", "c"), None, None),
            P(("dp", "y", "x", "c"), None, None),
            P(("dp", "y", "x", "c"), None, None),
            P(("dp", "y", "x", "c"), None, None),
            P(("dp", "y", "x", "c"), None, None),
            P(("dp", "y", "x", "c"), None, None),
            P(("dp", "y", "x", "c"), None, None),
            P(("dp", "y", "x", "c"), None),
            P(("dp", "y", "x", "c")),
            P(("dp", "y", "x", "c"), None, None),
            P(("y", "x", "c"), None),
            P(),
            P(("dp", "y", "x", "c"), None, None),
            P(("dp", "y", "x", "c"), None, None),
            P(("dp", "y", "x", "c"), None, None),
            P(("dp", "y", "x", "c"), None, None),
        ),
        out_specs=(P(("dp", "y", "x", "c"), None, None), P(("dp", "y", "x", "c"), None, None)),
        check_vma=False,
    )
```

```python
import functools
import math

import jax
import jax.numpy as jnp
from jax import lax
from jax.experimental import pallas as pl
from jax.experimental.pallas import tpu as pltpu
from jax.sharding import PartitionSpec as P

EPS = 1e-06


def decode_attention(queries, keys_new, values_new, importance, merge_flags, key_cache,
                     value_cache, last_weight, lengths):
    requests, steps, query_width = queries.shape
    heads_kv = last_weight.shape[1]
    slots, features = key_cache.shape[1], key_cache.shape[2]
    head_dim = features // heads_kv
    group = query_width // head_dim // heads_kv
    scale = 1.0 / math.sqrt(head_dim)
    f32, bf16 = jnp.float32, jnp.bfloat16

    chunk = math.gcd(slots, 128)
    window = 16

    chunks = slots // chunk

    def kernel(len_ref, flag_ref, share_ref, weight_ref, q_ref, kn_ref, vn_ref, k_hbm, v_hbm, o_ref,
               k_buf, v_buf, sems):
        r = pl.program_id(0)
        n = len_ref[r]
        here_buf = r % 2

        def copies(req, buf):
            needed = (len_ref[req] - 1) // chunk + 1
            for c in range(chunks):
                part = pl.ds(c * chunk, chunk)
                for a, (src, dst) in enumerate(((k_hbm, k_buf), (v_hbm, v_buf))):
                    copy = pltpu.make_async_copy(
                        src.at[req, part], dst.at[buf, part], sems.at[a, buf, c]
                    )
                    yield c < needed, copy

        def start_all(req, buf):
            for cond, copy in copies(req, buf):
                pl.when(cond)(copy.start)

        @pl.when(r == 0)
        def _():
            start_all(0, 0)

        @pl.when(r + 1 < requests)
        def _():
            start_all(r + 1, 1 - here_buf)

        for cond, copy in copies(r, here_buf):
            pl.when(cond)(copy.wait)
        k_ref = k_buf.at[here_buf]
        v_ref = v_buf.at[here_buf]
        start = pl.multiple_of(((n - 1) // window) * window, window)
        here = lax.broadcasted_iota(jnp.int32, (window, features), 0) == (n - 1 - start)
        last_k = jnp.sum(
            jnp.where(here, k_ref[pl.ds(start, window), :].astype(f32), 0.0), axis=0, keepdims=True
        )
        last_v = jnp.sum(
            jnp.where(here, v_ref[pl.ds(start, window), :].astype(f32), 0.0), axis=0, keepdims=True
        )
        new_k = kn_ref[0].astype(f32)
        new_v = vn_ref[0].astype(f32)

        def lane_mask(flag):
            return jnp.full((1, head_dim), flag, jnp.int32) == 1

        def row_mask(flag):
            return jnp.full((group, 1), flag, jnp.int32) == 1

        tails_of = []
        for g in range(heads_kv):
            lanes = slice(g * head_dim, (g + 1) * head_dim)
            z = weight_ref[r * heads_kv + g]
            f0 = flag_ref[(r * steps) * heads_kv + g]
            f1 = flag_ref[(r * steps + 1) * heads_kv + g]
            w0 = share_ref[(r * steps) * heads_kv + g]
            w1 = share_ref[(r * steps + 1) * heads_kv + g]
            z1 = jnp.where(f0 == 1, z + w0, w0)
            m0, m1 = lane_mask(f0), lane_mask(f1)
            both = lane_mask(f0 * f1)

            def settle(last, new):
                old0 = last[:, lanes]
                n0, n1 = new[0:1, lanes], new[1:2, lanes]
                b0 = ((z * old0 + w0 * n0) / (z + w0)).astype(bf16).astype(f32)
                a0 = jnp.where(m0, b0, old0)
                cur = jnp.where(m0, a0, n0)
                b1 = ((z1 * cur + w1 * n1) / (z1 + w1)).astype(bf16).astype(f32)
                second = (
                    jnp.where(both, b1, jnp.where(m0, a0, old0)),
                    jnp.where(m0, n1, jnp.where(m1, b1, n0)),
                    n1,
                )
                return (a0, n0), second

            count0 = 2 - f0
            tails_of.append((settle(last_k, new_k), settle(last_v, new_v), (count0, count0 + 1 - f1)))

        def attend(span):
            valid = lax.broadcasted_iota(jnp.int32, (steps * group, span), 1) < n - 1
            for g in range(heads_kv):
                lanes = slice(g * head_dim, (g + 1) * head_dim)
                keys_t, values_t, counts = tails_of[g]
                rows = slice(g * group, (g + 1) * group)
                q = jnp.concatenate([q_ref[0, t, rows, :] for t in range(steps)], axis=0)
                main = (
                    lax.dot_general(
                        q, k_ref[0:span, lanes], (((1,), (1,)), ((), ())),
                        preferred_element_type=f32,
                    )
                    * scale
                )
                main = jnp.where(valid, main, -jnp.inf)
                qf = q.astype(f32)
                top = jnp.max(main, axis=1, keepdims=True)
                tops, tails = [], []
                for t in range(steps):
                    here_rows = slice(t * group, (t + 1) * group)
                    top_t = top[here_rows]
                    step_tails = []
                    for j, (tk, tv) in enumerate(zip(keys_t[t], values_t[t])):
                        ts = jnp.sum(qf[here_rows] * tk, axis=1, keepdims=True) * scale
                        ts = jnp.where(row_mask((j < counts[t]).astype(jnp.int32)), ts, -jnp.inf)
                        top_t = jnp.maximum(top_t, ts)
                        step_tails.append((ts, tv))
                    tops.append(top_t)
                    tails.append(step_tails)
                top = jnp.concatenate(tops, axis=0)
                raw = jnp.exp(main - top)
                total = jnp.sum(raw, axis=1, keepdims=True)
                summed = jnp.dot(
                    raw.astype(bf16), v_ref[0:span, lanes], preferred_element_type=f32
                )
                for t in range(steps):
                    here_rows = slice(t * group, (t + 1) * group)
                    total_t = total[here_rows]
                    summed_t = summed[here_rows]
                    for ts, tv in tails[t]:
                        part = jnp.exp(ts - tops[t])
                        total_t = total_t + part
                        summed_t = summed_t + part.astype(bf16).astype(f32) * tv
                    o_ref[0, t, rows, :] = (summed_t / total_t).astype(bf16)

        used = (n - 1) // chunk + 1
        for k in range(1, slots // chunk + 1):
            pl.when(used == k)(functools.partial(attend, k * chunk))

    heads = query_width // head_dim
    per_query = pl.BlockSpec((1, steps, heads, head_dim), lambda r, *_: (r, 0, 0, 0))
    per_new = pl.BlockSpec((1, steps, features), lambda r, *_: (r, 0, 0))
    per_cache = pl.BlockSpec(memory_space=pl.ANY)
    out = pl.pallas_call(
        kernel,
        out_shape=jax.ShapeDtypeStruct((requests, steps, heads, head_dim), bf16),
        grid_spec=pltpu.PrefetchScalarGridSpec(
            num_scalar_prefetch=4,
            grid=(requests,),
            in_specs=[per_query, per_new, per_new, per_cache, per_cache],
            out_specs=per_query,
            scratch_shapes=[
                pltpu.VMEM((2, slots, features), key_cache.dtype),
                pltpu.VMEM((2, slots, features), value_cache.dtype),
                pltpu.SemaphoreType.DMA((2, 2, chunks)),
            ],
        ),
    )(
        lengths,
        merge_flags.reshape(-1),
        importance.reshape(-1),
        last_weight.reshape(-1),
        queries.reshape(requests, steps, heads, head_dim),
        keys_new,
        values_new,
        key_cache,
        value_cache,
    )
    return out.reshape(requests, steps, query_width)


def run_experts(arriving, expert_gate_up, expert_down):
    hidden_units = expert_down.shape[1]
    both = jnp.einsum(
        "sjcd,jdf->sjcf", arriving, expert_gate_up, preferred_element_type=jnp.float32
    )
    active = (jax.nn.silu(both[..., :hidden_units]) * both[..., hidden_units:]).astype(jnp.bfloat16)
    return jnp.einsum(
        "sjcf,jfd->sjcd", active, expert_down, preferred_element_type=jnp.float32
    ).astype(jnp.bfloat16)


def shards(
    queries,
    keys_new,
    values_new,
    importance,
    merge_flags,
    key_cache,
    value_cache,
    last_weight,
    lengths,
    residual,
    o_weight,
    norm_gain,
    expert_gate_up,
    expert_down,
    routes,
    route_weights,
):
    requests, steps, query_width = queries.shape
    attended = decode_attention(
        queries,
        keys_new,
        values_new,
        importance,
        merge_flags,
        key_cache,
        value_cache,
        last_weight,
        lengths,
    )
    rows = requests * steps
    width = o_weight.shape[1]
    gathered = lax.all_gather(o_weight, ("x", "c"), axis=0, tiled=True)
    lines = lax.axis_size("y")
    line = lax.axis_index("y")
    block = query_width // lines
    flat = attended.reshape(rows, query_width)

    def shifted(value, shift):
        return lax.ppermute(value, "y", [(j, (j + shift) % lines) for j in range(lines)])

    pieces = [lax.dynamic_slice_in_dim(flat, line * block, block, 1)]
    for shift in range(1, lines):
        piece = lax.dynamic_slice_in_dim(flat, ((line + shift) % lines) * block, block, 1)
        pieces.append(shifted(piece, shift))
    partials = jnp.dot(
        jnp.concatenate(pieces, axis=0), gathered, preferred_element_type=jnp.float32
    ).reshape(lines, rows, width)
    projected = partials[0]
    for shift in range(1, lines):
        projected = projected + shifted(partials[shift], lines - shift)
    members = lax.axis_size("y") * lax.axis_size("x") * lax.axis_size("c")
    mixed = residual.reshape(rows, width).astype(jnp.float32) + projected
    normed = (
        mixed * lax.rsqrt(jnp.mean(mixed * mixed, axis=1, keepdims=True) + EPS) * norm_gain
    ).astype(jnp.bfloat16)
    experts_local = expert_gate_up.shape[0]
    dp_size = lax.axis_size("dp")
    experts_all = experts_local * dp_size * members
    top_k = routes.shape[2]
    capacity = max(2, 2 * rows * top_k // experts_all)
    chosen = routes.reshape(rows * top_k)
    sequence = jnp.arange(rows * top_k, dtype=jnp.int32)
    earlier = sequence[:, None] > sequence[None, :]
    rank = jnp.sum(((chosen[:, None] == chosen[None, :]) & earlier).astype(jnp.int32), axis=1)
    target = chosen * capacity + rank
    placing = (
        jnp.arange(experts_all * capacity, dtype=jnp.int32)[:, None] == target[None, :]
    ).reshape(experts_all * capacity, rows, top_k)
    placing = jnp.any(placing, axis=2).astype(jnp.bfloat16)
    outgoing = jnp.dot(placing, normed, preferred_element_type=jnp.float32).astype(jnp.bfloat16)
    ep_axes = ("y", "x", "c")
    arrived = lax.all_to_all(
        outgoing.reshape(dp_size, members, capacity, width), "dp", 0, 0, tiled=True
    )
    arrived = lax.all_to_all(arrived, ep_axes, 1, 1, tiled=True).reshape(
        experts_all, capacity, width
    )
    depth = arrived.shape[1]
    sources = arrived.shape[0] // experts_local
    answer = run_experts(
        arrived.reshape(sources, experts_local, depth, width), expert_gate_up, expert_down
    )
    returned = lax.all_to_all(
        answer.reshape(dp_size, members, depth, width), ep_axes, 1, 1, tiled=True
    )
    returned = lax.all_to_all(returned, "dp", 0, 0, tiled=True)
    slots_all = jnp.arange(experts_all * capacity, dtype=jnp.int32)
    gathering = jnp.sum(
        jnp.where(
            slots_all[None, None, :] == target.reshape(rows, top_k, 1),
            route_weights.reshape(rows, top_k, 1),
            0.0,
        ),
        axis=1,
    )
    blended = jnp.dot(
        gathering,
        returned.reshape(experts_all * capacity, width).astype(jnp.float32),
        precision=lax.Precision.HIGHEST,
        preferred_element_type=jnp.float32,
    )
    layer_out = (mixed + blended).astype(jnp.bfloat16).reshape(requests, steps, width)
    return (attended, layer_out)


def solution(mesh):
    lines = mesh.devices.shape[1] // 8
    mesh = jax.sharding.Mesh(
        mesh.devices.reshape(mesh.devices.shape[0], lines, 4, 2), ("dp", "y", "x", "c")
    )
    return jax.shard_map(
        shards,
        mesh=mesh,
        in_specs=(
            P(("dp", "y", "x", "c"), None, None),
            P(("dp", "y", "x", "c"), None, None),
            P(("dp", "y", "x", "c"), None, None),
            P(("dp", "y", "x", "c"), None, None),
            P(("dp", "y", "x", "c"), None, None),
            P(("dp", "y", "x", "c"), None, None),
            P(("dp", "y", "x", "c"), None, None),
            P(("dp", "y", "x", "c"), None),
            P(("dp", "y", "x", "c")),
            P(("dp", "y", "x", "c"), None, None),
            P(("y", "x", "c"), None),
            P(),
            P(("dp", "y", "x", "c"), None, None),
            P(("dp", "y", "x", "c"), None, None),
            P(("dp", "y", "x", "c"), None, None),
            P(("dp", "y", "x", "c"), None, None),
        ),
        out_specs=(P(("dp", "y", "x", "c"), None, None), P(("dp", "y", "x", "c"), None, None)),
        check_vma=False,
    )
```

```python
import functools
import math

import jax
import jax.numpy as jnp
from jax import lax
from jax.experimental import pallas as pl
from jax.experimental.pallas import tpu as pltpu
from jax.sharding import PartitionSpec as P

EPS = 1e-06


def decode_attention(queries, keys_new, values_new, importance, merge_flags, key_cache,
                     value_cache, last_weight, lengths):
    requests, steps, query_width = queries.shape
    heads_kv = last_weight.shape[1]
    slots, features = key_cache.shape[1], key_cache.shape[2]
    head_dim = features // heads_kv
    group = query_width // head_dim // heads_kv
    scale = 1.0 / math.sqrt(head_dim)
    f32, bf16 = jnp.float32, jnp.bfloat16

    chunk = math.gcd(slots, 128)
    window = 16

    chunks = slots // chunk

    def kernel(len_ref, flag_ref, share_ref, weight_ref, q_ref, kn_ref, vn_ref, k_hbm, v_hbm, o_ref,
               k_buf, v_buf, sems):
        r = pl.program_id(0)
        n = len_ref[r]
        here_buf = r % 2

        def copies(req, buf):
            needed = (len_ref[req] - 1) // chunk + 1
            for c in range(chunks):
                part = pl.ds(c * chunk, chunk)
                for a, (src, dst) in enumerate(((k_hbm, k_buf), (v_hbm, v_buf))):
                    copy = pltpu.make_async_copy(
                        src.at[req, part], dst.at[buf, part], sems.at[a, buf, c]
                    )
                    yield c < needed, copy

        def start_all(req, buf):
            for cond, copy in copies(req, buf):
                pl.when(cond)(copy.start)

        @pl.when(r == 0)
        def _():
            start_all(0, 0)

        @pl.when(r + 1 < requests)
        def _():
            start_all(r + 1, 1 - here_buf)

        for cond, copy in copies(r, here_buf):
            pl.when(cond)(copy.wait)
        k_ref = k_buf.at[here_buf]
        v_ref = v_buf.at[here_buf]
        start = pl.multiple_of(((n - 1) // window) * window, window)
        here = lax.broadcasted_iota(jnp.int32, (window, features), 0) == (n - 1 - start)
        last_k = jnp.sum(
            jnp.where(here, k_ref[pl.ds(start, window), :].astype(f32), 0.0), axis=0, keepdims=True
        )
        last_v = jnp.sum(
            jnp.where(here, v_ref[pl.ds(start, window), :].astype(f32), 0.0), axis=0, keepdims=True
        )
        new_k = kn_ref[0].astype(f32)
        new_v = vn_ref[0].astype(f32)

        def lane_mask(flag):
            return jnp.full((1, head_dim), flag, jnp.int32) == 1

        def row_mask(flag):
            return jnp.full((group, 1), flag, jnp.int32) == 1

        tails_of = []
        for g in range(heads_kv):
            lanes = slice(g * head_dim, (g + 1) * head_dim)
            z = weight_ref[r * heads_kv + g]
            f0 = flag_ref[(r * steps) * heads_kv + g]
            f1 = flag_ref[(r * steps + 1) * heads_kv + g]
            w0 = share_ref[(r * steps) * heads_kv + g]
            w1 = share_ref[(r * steps + 1) * heads_kv + g]
            z1 = jnp.where(f0 == 1, z + w0, w0)
            m0, m1 = lane_mask(f0), lane_mask(f1)
            both = lane_mask(f0 * f1)

            def settle(last, new):
                old0 = last[:, lanes]
                n0, n1 = new[0:1, lanes], new[1:2, lanes]
                b0 = ((z * old0 + w0 * n0) / (z + w0)).astype(bf16).astype(f32)
                a0 = jnp.where(m0, b0, old0)
                cur = jnp.where(m0, a0, n0)
                b1 = ((z1 * cur + w1 * n1) / (z1 + w1)).astype(bf16).astype(f32)
                second = (
                    jnp.where(both, b1, jnp.where(m0, a0, old0)),
                    jnp.where(m0, n1, jnp.where(m1, b1, n0)),
                    n1,
                )
                return (a0, n0), second

            count0 = 2 - f0
            tails_of.append((settle(last_k, new_k), settle(last_v, new_v), (count0, count0 + 1 - f1)))

        def attend(span):
            valid = lax.broadcasted_iota(jnp.int32, (steps * group, span), 1) < n - 1
            for g in range(heads_kv):
                lanes = slice(g * head_dim, (g + 1) * head_dim)
                keys_t, values_t, counts = tails_of[g]
                rows = slice(g * group, (g + 1) * group)
                q = jnp.concatenate([q_ref[0, t, rows, :] for t in range(steps)], axis=0)
                main = (
                    lax.dot_general(
                        q, k_ref[0:span, lanes], (((1,), (1,)), ((), ())),
                        preferred_element_type=f32,
                    )
                    * scale
                )
                main = jnp.where(valid, main, -jnp.inf)
                qf = q.astype(f32)
                top = jnp.max(main, axis=1, keepdims=True)
                tops, tails = [], []
                for t in range(steps):
                    here_rows = slice(t * group, (t + 1) * group)
                    top_t = top[here_rows]
                    step_tails = []
                    for j, (tk, tv) in enumerate(zip(keys_t[t], values_t[t])):
                        ts = jnp.sum(qf[here_rows] * tk, axis=1, keepdims=True) * scale
                        ts = jnp.where(row_mask((j < counts[t]).astype(jnp.int32)), ts, -jnp.inf)
                        top_t = jnp.maximum(top_t, ts)
                        step_tails.append((ts, tv))
                    tops.append(top_t)
                    tails.append(step_tails)
                top = jnp.concatenate(tops, axis=0)
                raw = jnp.exp(main - top)
                total = jnp.sum(raw, axis=1, keepdims=True)
                summed = jnp.dot(
                    raw.astype(bf16), v_ref[0:span, lanes], preferred_element_type=f32
                )
                for t in range(steps):
                    here_rows = slice(t * group, (t + 1) * group)
                    total_t = total[here_rows]
                    summed_t = summed[here_rows]
                    for ts, tv in tails[t]:
                        part = jnp.exp(ts - tops[t])
                        total_t = total_t + part
                        summed_t = summed_t + part.astype(bf16).astype(f32) * tv
                    o_ref[0, t, rows, :] = (summed_t / total_t).astype(bf16)

        used = (n - 1) // chunk + 1
        for k in range(1, slots // chunk + 1):
            pl.when(used == k)(functools.partial(attend, k * chunk))

    heads = query_width // head_dim
    per_query = pl.BlockSpec((1, steps, heads, head_dim), lambda r, *_: (r, 0, 0, 0))
    per_new = pl.BlockSpec((1, steps, features), lambda r, *_: (r, 0, 0))
    per_cache = pl.BlockSpec(memory_space=pl.ANY)
    out = pl.pallas_call(
        kernel,
        out_shape=jax.ShapeDtypeStruct((requests, steps, heads, head_dim), bf16),
        grid_spec=pltpu.PrefetchScalarGridSpec(
            num_scalar_prefetch=4,
            grid=(requests,),
            in_specs=[per_query, per_new, per_new, per_cache, per_cache],
            out_specs=per_query,
            scratch_shapes=[
                pltpu.VMEM((2, slots, features), key_cache.dtype),
                pltpu.VMEM((2, slots, features), value_cache.dtype),
                pltpu.SemaphoreType.DMA((2, 2, chunks)),
            ],
        ),
    )(
        lengths,
        merge_flags.reshape(-1),
        importance.reshape(-1),
        last_weight.reshape(-1),
        queries.reshape(requests, steps, heads, head_dim),
        keys_new,
        values_new,
        key_cache,
        value_cache,
    )
    return out.reshape(requests, steps, query_width)


def run_experts(arriving, expert_gate_up, expert_down):
    hidden_units = expert_down.shape[1]
    both = jnp.einsum(
        "sjcd,jdf->sjcf", arriving, expert_gate_up, preferred_element_type=jnp.float32
    )
    active = (jax.nn.silu(both[..., :hidden_units]) * both[..., hidden_units:]).astype(jnp.bfloat16)
    return jnp.einsum(
        "sjcf,jfd->sjcd", active, expert_down, preferred_element_type=jnp.float32
    ).astype(jnp.bfloat16)


def shards(
    queries,
    keys_new,
    values_new,
    importance,
    merge_flags,
    key_cache,
    value_cache,
    last_weight,
    lengths,
    residual,
    o_weight,
    norm_gain,
    expert_gate_up,
    expert_down,
    routes,
    route_weights,
):
    requests, steps, query_width = queries.shape
    attended = decode_attention(
        queries,
        keys_new,
        values_new,
        importance,
        merge_flags,
        key_cache,
        value_cache,
        last_weight,
        lengths,
    )
    rows = requests * steps
    width = o_weight.shape[1]
    gathered = lax.all_gather(o_weight, ("x", "c"), axis=0, tiled=True)
    lines = lax.axis_size("y")
    line = lax.axis_index("y")
    block = query_width // lines
    flat = attended.reshape(rows, query_width)

    def shifted(value, shift):
        return lax.ppermute(value, "y", [(j, (j + shift) % lines) for j in range(lines)])

    pieces = [lax.dynamic_slice_in_dim(flat, line * block, block, 1)]
    for shift in range(1, lines):
        piece = lax.dynamic_slice_in_dim(flat, ((line + shift) % lines) * block, block, 1)
        pieces.append(shifted(piece, shift))
    partials = jnp.dot(
        jnp.concatenate(pieces, axis=0), gathered, preferred_element_type=jnp.float32
    ).reshape(lines, rows, width)
    projected = partials[0]
    for shift in range(1, lines):
        sent = shifted(partials[shift].astype(jnp.bfloat16), lines - shift)
        projected = projected + sent.astype(jnp.float32)
    members = lax.axis_size("y") * lax.axis_size("x") * lax.axis_size("c")
    mixed = residual.reshape(rows, width).astype(jnp.float32) + projected
    normed = (
        mixed * lax.rsqrt(jnp.mean(mixed * mixed, axis=1, keepdims=True) + EPS) * norm_gain
    ).astype(jnp.bfloat16)
    experts_local = expert_gate_up.shape[0]
    dp_size = lax.axis_size("dp")
    experts_all = experts_local * dp_size * members
    top_k = routes.shape[2]
    capacity = max(2, 2 * rows * top_k // experts_all)
    chosen = routes.reshape(rows * top_k)
    sequence = jnp.arange(rows * top_k, dtype=jnp.int32)
    earlier = sequence[:, None] > sequence[None, :]
    rank = jnp.sum(((chosen[:, None] == chosen[None, :]) & earlier).astype(jnp.int32), axis=1)
    target = chosen * capacity + rank
    placing = (
        jnp.arange(experts_all * capacity, dtype=jnp.int32)[:, None] == target[None, :]
    ).reshape(experts_all * capacity, rows, top_k)
    placing = jnp.any(placing, axis=2).astype(jnp.bfloat16)
    outgoing = jnp.dot(placing, normed, preferred_element_type=jnp.float32).astype(jnp.bfloat16)
    arrived = lax.all_to_all(
        outgoing.reshape(experts_all, capacity, width),
        ("dp", "y", "x", "c"),
        split_axis=0,
        concat_axis=0,
        tiled=True,
    )
    depth = arrived.shape[1]
    sources = arrived.shape[0] // experts_local
    answer = run_experts(
        arrived.reshape(sources, experts_local, depth, width), expert_gate_up, expert_down
    )
    returned = lax.all_to_all(
        answer.reshape(sources * experts_local, depth, width),
        ("dp", "y", "x", "c"),
        split_axis=0,
        concat_axis=0,
        tiled=True,
    )
    slots_all = jnp.arange(experts_all * capacity, dtype=jnp.int32)
    gathering = jnp.sum(
        jnp.where(
            slots_all[None, None, :] == target.reshape(rows, top_k, 1),
            route_weights.reshape(rows, top_k, 1),
            0.0,
        ),
        axis=1,
    )
    blended = jnp.dot(
        gathering,
        returned.reshape(experts_all * capacity, width).astype(jnp.float32),
        precision=lax.Precision.HIGHEST,
        preferred_element_type=jnp.float32,
    )
    layer_out = (mixed + blended).astype(jnp.bfloat16).reshape(requests, steps, width)
    return (attended, layer_out)


def solution(mesh):
    lines = mesh.devices.shape[1] // 8
    mesh = jax.sharding.Mesh(
        mesh.devices.reshape(mesh.devices.shape[0], lines, 4, 2), ("dp", "y", "x", "c")
    )
    return jax.shard_map(
        shards,
        mesh=mesh,
        in_specs=(
            P(("dp", "y", "x", "c"), None, None),
            P(("dp", "y", "x", "c"), None, None),
            P(("dp", "y", "x", "c"), None, None),
            P(("dp", "y", "x", "c"), None, None),
            P(("dp", "y", "x", "c"), None, None),
            P(("dp", "y", "x", "c"), None, None),
            P(("dp", "y", "x", "c"), None, None),
            P(("dp", "y", "x", "c"), None),
            P(("dp", "y", "x", "c")),
            P(("dp", "y", "x", "c"), None, None),
            P(("y", "x", "c"), None),
            P(),
            P(("dp", "y", "x", "c"), None, None),
            P(("dp", "y", "x", "c"), None, None),
            P(("dp", "y", "x", "c"), None, None),
            P(("dp", "y", "x", "c"), None, None),
        ),
        out_specs=(P(("dp", "y", "x", "c"), None, None), P(("dp", "y", "x", "c"), None, None)),
        check_vma=False,
    )
```

```python
import functools
import math

import jax
import jax.numpy as jnp
from jax import lax
from jax.experimental import pallas as pl
from jax.experimental.pallas import tpu as pltpu
from jax.sharding import PartitionSpec as P

EPS = 1e-06


def decode_attention(queries, keys_new, values_new, importance, merge_flags, key_cache,
                     value_cache, last_weight, lengths):
    requests, steps, query_width = queries.shape
    heads_kv = last_weight.shape[1]
    slots, features = key_cache.shape[1], key_cache.shape[2]
    head_dim = features // heads_kv
    group = query_width // head_dim // heads_kv
    scale = 1.0 / math.sqrt(head_dim)
    f32, bf16 = jnp.float32, jnp.bfloat16

    chunk = math.gcd(slots, 128)
    window = 16

    chunks = slots // chunk

    def kernel(len_ref, flag_ref, share_ref, weight_ref, q_ref, kn_ref, vn_ref, k_hbm, v_hbm, o_ref,
               k_buf, v_buf, sems):
        r = pl.program_id(0)
        n = len_ref[r]
        here_buf = r % 2

        def copies(req, buf):
            needed = (len_ref[req] - 1) // chunk + 1
            for c in range(chunks):
                part = pl.ds(c * chunk, chunk)
                for a, (src, dst) in enumerate(((k_hbm, k_buf), (v_hbm, v_buf))):
                    copy = pltpu.make_async_copy(
                        src.at[req, part], dst.at[buf, part], sems.at[a, buf, c]
                    )
                    yield c < needed, copy

        def start_all(req, buf):
            for cond, copy in copies(req, buf):
                pl.when(cond)(copy.start)

        @pl.when(r == 0)
        def _():
            start_all(0, 0)

        @pl.when(r + 1 < requests)
        def _():
            start_all(r + 1, 1 - here_buf)

        for cond, copy in copies(r, here_buf):
            pl.when(cond)(copy.wait)
        k_ref = k_buf.at[here_buf]
        v_ref = v_buf.at[here_buf]
        start = pl.multiple_of(((n - 1) // window) * window, window)
        here = lax.broadcasted_iota(jnp.int32, (window, features), 0) == (n - 1 - start)
        last_k = jnp.sum(
            jnp.where(here, k_ref[pl.ds(start, window), :].astype(f32), 0.0), axis=0, keepdims=True
        )
        last_v = jnp.sum(
            jnp.where(here, v_ref[pl.ds(start, window), :].astype(f32), 0.0), axis=0, keepdims=True
        )
        new_k = kn_ref[0].astype(f32)
        new_v = vn_ref[0].astype(f32)

        def lane_mask(flag):
            return jnp.full((1, head_dim), flag, jnp.int32) == 1

        def row_mask(flag):
            return jnp.full((group, 1), flag, jnp.int32) == 1

        tails_of = []
        for g in range(heads_kv):
            lanes = slice(g * head_dim, (g + 1) * head_dim)
            z = weight_ref[r * heads_kv + g]
            f0 = flag_ref[(r * steps) * heads_kv + g]
            f1 = flag_ref[(r * steps + 1) * heads_kv + g]
            w0 = share_ref[(r * steps) * heads_kv + g]
            w1 = share_ref[(r * steps + 1) * heads_kv + g]
            z1 = jnp.where(f0 == 1, z + w0, w0)
            m0, m1 = lane_mask(f0), lane_mask(f1)
            both = lane_mask(f0 * f1)

            def settle(last, new):
                old0 = last[:, lanes]
                n0, n1 = new[0:1, lanes], new[1:2, lanes]
                b0 = ((z * old0 + w0 * n0) / (z + w0)).astype(bf16).astype(f32)
                a0 = jnp.where(m0, b0, old0)
                cur = jnp.where(m0, a0, n0)
                b1 = ((z1 * cur + w1 * n1) / (z1 + w1)).astype(bf16).astype(f32)
                second = (
                    jnp.where(both, b1, jnp.where(m0, a0, old0)),
                    jnp.where(m0, n1, jnp.where(m1, b1, n0)),
                    n1,
                )
                return (a0, n0), second

            count0 = 2 - f0
            tails_of.append((settle(last_k, new_k), settle(last_v, new_v), (count0, count0 + 1 - f1)))

        def attend(span):
            valid = lax.broadcasted_iota(jnp.int32, (steps * group, span), 1) < n - 1
            for g in range(heads_kv):
                lanes = slice(g * head_dim, (g + 1) * head_dim)
                keys_t, values_t, counts = tails_of[g]
                rows = slice(g * group, (g + 1) * group)
                q = jnp.concatenate([q_ref[0, t, rows, :] for t in range(steps)], axis=0)
                main = (
                    lax.dot_general(
                        q, k_ref[0:span, lanes], (((1,), (1,)), ((), ())),
                        preferred_element_type=f32,
                    )
                    * scale
                )
                main = jnp.where(valid, main, -jnp.inf)
                qf = q.astype(f32)
                top = jnp.max(main, axis=1, keepdims=True)
                tops, tails = [], []
                for t in range(steps):
                    here_rows = slice(t * group, (t + 1) * group)
                    top_t = top[here_rows]
                    step_tails = []
                    for j, (tk, tv) in enumerate(zip(keys_t[t], values_t[t])):
                        ts = jnp.sum(qf[here_rows] * tk, axis=1, keepdims=True) * scale
                        ts = jnp.where(row_mask((j < counts[t]).astype(jnp.int32)), ts, -jnp.inf)
                        top_t = jnp.maximum(top_t, ts)
                        step_tails.append((ts, tv))
                    tops.append(top_t)
                    tails.append(step_tails)
                top = jnp.concatenate(tops, axis=0)
                raw = jnp.exp(main - top)
                total = jnp.sum(raw, axis=1, keepdims=True)
                summed = jnp.dot(
                    raw.astype(bf16), v_ref[0:span, lanes], preferred_element_type=f32
                )
                for t in range(steps):
                    here_rows = slice(t * group, (t + 1) * group)
                    total_t = total[here_rows]
                    summed_t = summed[here_rows]
                    for ts, tv in tails[t]:
                        part = jnp.exp(ts - tops[t])
                        total_t = total_t + part
                        summed_t = summed_t + part.astype(bf16).astype(f32) * tv
                    o_ref[0, t, rows, :] = (summed_t / total_t).astype(bf16)

        used = (n - 1) // chunk + 1
        for k in range(1, slots // chunk + 1):
            pl.when(used == k)(functools.partial(attend, k * chunk))

    heads = query_width // head_dim
    per_query = pl.BlockSpec((1, steps, heads, head_dim), lambda r, *_: (r, 0, 0, 0))
    per_new = pl.BlockSpec((1, steps, features), lambda r, *_: (r, 0, 0))
    per_cache = pl.BlockSpec(memory_space=pl.ANY)
    out = pl.pallas_call(
        kernel,
        out_shape=jax.ShapeDtypeStruct((requests, steps, heads, head_dim), bf16),
        grid_spec=pltpu.PrefetchScalarGridSpec(
            num_scalar_prefetch=4,
            grid=(requests,),
            in_specs=[per_query, per_new, per_new, per_cache, per_cache],
            out_specs=per_query,
            scratch_shapes=[
                pltpu.VMEM((2, slots, features), key_cache.dtype),
                pltpu.VMEM((2, slots, features), value_cache.dtype),
                pltpu.SemaphoreType.DMA((2, 2, chunks)),
            ],
        ),
    )(
        lengths,
        merge_flags.reshape(-1),
        importance.reshape(-1),
        last_weight.reshape(-1),
        queries.reshape(requests, steps, heads, head_dim),
        keys_new,
        values_new,
        key_cache,
        value_cache,
    )
    return out.reshape(requests, steps, query_width)


def run_experts(arriving, expert_gate_up, expert_down):
    hidden_units = expert_down.shape[1]
    both = jnp.einsum(
        "sjcd,jdf->sjcf", arriving, expert_gate_up, preferred_element_type=jnp.float32
    )
    active = (jax.nn.silu(both[..., :hidden_units]) * both[..., hidden_units:]).astype(jnp.bfloat16)
    return jnp.einsum(
        "sjcf,jfd->sjcd", active, expert_down, preferred_element_type=jnp.float32
    ).astype(jnp.bfloat16)


def shards(
    queries,
    keys_new,
    values_new,
    importance,
    merge_flags,
    key_cache,
    value_cache,
    last_weight,
    lengths,
    residual,
    o_weight,
    norm_gain,
    expert_gate_up,
    expert_down,
    routes,
    route_weights,
):
    requests, steps, query_width = queries.shape
    attended = decode_attention(
        queries,
        keys_new,
        values_new,
        importance,
        merge_flags,
        key_cache,
        value_cache,
        last_weight,
        lengths,
    )
    rows = requests * steps
    width = o_weight.shape[1]
    gathered = lax.all_gather(o_weight, ("xl", "c"), axis=0, tiled=True)
    across = ("y", "xh")
    lines = lax.axis_size(across)
    line = lax.axis_index(across)
    block = query_width // lines
    flat = attended.reshape(rows, query_width)

    def shifted(value, shift):
        return lax.ppermute(value, across, [(j, (j + shift) % lines) for j in range(lines)])

    pieces = [lax.dynamic_slice_in_dim(flat, line * block, block, 1)]
    for shift in range(1, lines):
        piece = lax.dynamic_slice_in_dim(flat, ((line + shift) % lines) * block, block, 1)
        pieces.append(shifted(piece, shift))
    partials = jnp.dot(
        jnp.concatenate(pieces, axis=0), gathered, preferred_element_type=jnp.float32
    ).reshape(lines, rows, width)
    projected = partials[0]
    for shift in range(1, lines):
        sent = shifted(partials[shift].astype(jnp.bfloat16), lines - shift)
        projected = projected + sent.astype(jnp.float32)
    members = lax.axis_size(("y", "xh", "xl", "c"))
    mixed = residual.reshape(rows, width).astype(jnp.float32) + projected
    normed = (
        mixed * lax.rsqrt(jnp.mean(mixed * mixed, axis=1, keepdims=True) + EPS) * norm_gain
    ).astype(jnp.bfloat16)
    experts_local = expert_gate_up.shape[0]
    dp_size = lax.axis_size("dp")
    experts_all = experts_local * dp_size * members
    top_k = routes.shape[2]
    capacity = max(2, 2 * rows * top_k // experts_all)
    chosen = routes.reshape(rows * top_k)
    sequence = jnp.arange(rows * top_k, dtype=jnp.int32)
    earlier = sequence[:, None] > sequence[None, :]
    rank = jnp.sum(((chosen[:, None] == chosen[None, :]) & earlier).astype(jnp.int32), axis=1)
    target = chosen * capacity + rank
    placing = (
        jnp.arange(experts_all * capacity, dtype=jnp.int32)[:, None] == target[None, :]
    ).reshape(experts_all * capacity, rows, top_k)
    placing = jnp.any(placing, axis=2).astype(jnp.bfloat16)
    outgoing = jnp.dot(placing, normed, preferred_element_type=jnp.float32).astype(jnp.bfloat16)
    arrived = lax.all_to_all(
        outgoing.reshape(experts_all, capacity, width),
        ("dp", "y", "xh", "xl", "c"),
        split_axis=0,
        concat_axis=0,
        tiled=True,
    )
    depth = arrived.shape[1]
    sources = arrived.shape[0] // experts_local
    answer = run_experts(
        arrived.reshape(sources, experts_local, depth, width), expert_gate_up, expert_down
    )
    returned = lax.all_to_all(
        answer.reshape(sources * experts_local, depth, width),
        ("dp", "y", "xh", "xl", "c"),
        split_axis=0,
        concat_axis=0,
        tiled=True,
    )
    slots_all = jnp.arange(experts_all * capacity, dtype=jnp.int32)
    gathering = jnp.sum(
        jnp.where(
            slots_all[None, None, :] == target.reshape(rows, top_k, 1),
            route_weights.reshape(rows, top_k, 1),
            0.0,
        ),
        axis=1,
    )
    blended = jnp.dot(
        gathering,
        returned.reshape(experts_all * capacity, width).astype(jnp.float32),
        precision=lax.Precision.HIGHEST,
        preferred_element_type=jnp.float32,
    )
    layer_out = (mixed + blended).astype(jnp.bfloat16).reshape(requests, steps, width)
    return (attended, layer_out)


def solution(mesh):
    lines = mesh.devices.shape[1] // 8
    mesh = jax.sharding.Mesh(
        mesh.devices.reshape(mesh.devices.shape[0], lines, 2, 2, 2), ("dp", "y", "xh", "xl", "c")
    )
    return jax.shard_map(
        shards,
        mesh=mesh,
        in_specs=(
            P(("dp", "y", "xh", "xl", "c"), None, None),
            P(("dp", "y", "xh", "xl", "c"), None, None),
            P(("dp", "y", "xh", "xl", "c"), None, None),
            P(("dp", "y", "xh", "xl", "c"), None, None),
            P(("dp", "y", "xh", "xl", "c"), None, None),
            P(("dp", "y", "xh", "xl", "c"), None, None),
            P(("dp", "y", "xh", "xl", "c"), None, None),
            P(("dp", "y", "xh", "xl", "c"), None),
            P(("dp", "y", "xh", "xl", "c")),
            P(("dp", "y", "xh", "xl", "c"), None, None),
            P(("y", "xh", "xl", "c"), None),
            P(),
            P(("dp", "y", "xh", "xl", "c"), None, None),
            P(("dp", "y", "xh", "xl", "c"), None, None),
            P(("dp", "y", "xh", "xl", "c"), None, None),
            P(("dp", "y", "xh", "xl", "c"), None, None),
        ),
        out_specs=(P(("dp", "y", "xh", "xl", "c"), None, None), P(("dp", "y", "xh", "xl", "c"), None, None)),
        check_vma=False,
    )
```

```python
import functools
import math

import jax
import jax.numpy as jnp
from jax import lax
from jax.experimental import pallas as pl
from jax.experimental.pallas import tpu as pltpu
from jax.sharding import PartitionSpec as P

EPS = 1e-06


def decode_attention(queries, keys_new, values_new, importance, merge_flags, key_cache,
                     value_cache, last_weight, lengths):
    requests, steps, query_width = queries.shape
    heads_kv = last_weight.shape[1]
    slots, features = key_cache.shape[1], key_cache.shape[2]
    head_dim = features // heads_kv
    group = query_width // head_dim // heads_kv
    scale = 1.0 / math.sqrt(head_dim)
    f32, bf16 = jnp.float32, jnp.bfloat16

    chunk = math.gcd(slots, 128)
    window = 16

    chunks = slots // chunk

    def kernel(len_ref, flag_ref, share_ref, weight_ref, q_ref, kn_ref, vn_ref, k_hbm, v_hbm, o_ref,
               k_buf, v_buf, sems):
        r = pl.program_id(0)
        n = len_ref[r]
        here_buf = r % 2

        def copies(req, buf):
            needed = (len_ref[req] - 1) // chunk + 1
            for c in range(chunks):
                part = pl.ds(c * chunk, chunk)
                for a, (src, dst) in enumerate(((k_hbm, k_buf), (v_hbm, v_buf))):
                    copy = pltpu.make_async_copy(
                        src.at[req, part], dst.at[buf, part], sems.at[a, buf, c]
                    )
                    yield c < needed, copy

        def start_all(req, buf):
            for cond, copy in copies(req, buf):
                pl.when(cond)(copy.start)

        @pl.when(r == 0)
        def _():
            start_all(0, 0)

        @pl.when(r + 1 < requests)
        def _():
            start_all(r + 1, 1 - here_buf)

        for cond, copy in copies(r, here_buf):
            pl.when(cond)(copy.wait)
        k_ref = k_buf.at[here_buf]
        v_ref = v_buf.at[here_buf]
        start = pl.multiple_of(((n - 1) // window) * window, window)
        here = lax.broadcasted_iota(jnp.int32, (window, features), 0) == (n - 1 - start)
        last_k = jnp.sum(
            jnp.where(here, k_ref[pl.ds(start, window), :].astype(f32), 0.0), axis=0, keepdims=True
        )
        last_v = jnp.sum(
            jnp.where(here, v_ref[pl.ds(start, window), :].astype(f32), 0.0), axis=0, keepdims=True
        )
        new_k = kn_ref[0].astype(f32)
        new_v = vn_ref[0].astype(f32)

        def lane_mask(flag):
            return jnp.full((1, head_dim), flag, jnp.int32) == 1

        def row_mask(flag):
            return jnp.full((group, 1), flag, jnp.int32) == 1

        tails_of = []
        for g in range(heads_kv):
            lanes = slice(g * head_dim, (g + 1) * head_dim)
            z = weight_ref[r * heads_kv + g]
            f0 = flag_ref[(r * steps) * heads_kv + g]
            f1 = flag_ref[(r * steps + 1) * heads_kv + g]
            w0 = share_ref[(r * steps) * heads_kv + g]
            w1 = share_ref[(r * steps + 1) * heads_kv + g]
            z1 = jnp.where(f0 == 1, z + w0, w0)
            m0, m1 = lane_mask(f0), lane_mask(f1)
            both = lane_mask(f0 * f1)

            def settle(last, new):
                old0 = last[:, lanes]
                n0, n1 = new[0:1, lanes], new[1:2, lanes]
                b0 = ((z * old0 + w0 * n0) / (z + w0)).astype(bf16).astype(f32)
                a0 = jnp.where(m0, b0, old0)
                cur = jnp.where(m0, a0, n0)
                b1 = ((z1 * cur + w1 * n1) / (z1 + w1)).astype(bf16).astype(f32)
                second = (
                    jnp.where(both, b1, jnp.where(m0, a0, old0)),
                    jnp.where(m0, n1, jnp.where(m1, b1, n0)),
                    n1,
                )
                return (a0, n0), second

            count0 = 2 - f0
            tails_of.append((settle(last_k, new_k), settle(last_v, new_v), (count0, count0 + 1 - f1)))

        def attend(span):
            valid = lax.broadcasted_iota(jnp.int32, (steps * group, span), 1) < n - 1
            for g in range(heads_kv):
                lanes = slice(g * head_dim, (g + 1) * head_dim)
                keys_t, values_t, counts = tails_of[g]
                rows = slice(g * group, (g + 1) * group)
                q = jnp.concatenate([q_ref[0, t, rows, :] for t in range(steps)], axis=0)
                main = (
                    lax.dot_general(
                        q, k_ref[0:span, lanes], (((1,), (1,)), ((), ())),
                        preferred_element_type=f32,
                    )
                    * scale
                )
                main = jnp.where(valid, main, -jnp.inf)
                qf = q.astype(f32)
                top = jnp.max(main, axis=1, keepdims=True)
                tops, tails = [], []
                for t in range(steps):
                    here_rows = slice(t * group, (t + 1) * group)
                    top_t = top[here_rows]
                    step_tails = []
                    for j, (tk, tv) in enumerate(zip(keys_t[t], values_t[t])):
                        ts = jnp.sum(qf[here_rows] * tk, axis=1, keepdims=True) * scale
                        ts = jnp.where(row_mask((j < counts[t]).astype(jnp.int32)), ts, -jnp.inf)
                        top_t = jnp.maximum(top_t, ts)
                        step_tails.append((ts, tv))
                    tops.append(top_t)
                    tails.append(step_tails)
                top = jnp.concatenate(tops, axis=0)
                raw = jnp.exp(main - top)
                total = jnp.sum(raw, axis=1, keepdims=True)
                summed = jnp.dot(
                    raw.astype(bf16), v_ref[0:span, lanes], preferred_element_type=f32
                )
                for t in range(steps):
                    here_rows = slice(t * group, (t + 1) * group)
                    total_t = total[here_rows]
                    summed_t = summed[here_rows]
                    for ts, tv in tails[t]:
                        part = jnp.exp(ts - tops[t])
                        total_t = total_t + part
                        summed_t = summed_t + part.astype(bf16).astype(f32) * tv
                    o_ref[0, t, rows, :] = (summed_t / total_t).astype(bf16)

        used = (n - 1) // chunk + 1
        for k in range(1, slots // chunk + 1):
            pl.when(used == k)(functools.partial(attend, k * chunk))

    heads = query_width // head_dim
    per_query = pl.BlockSpec((1, steps, heads, head_dim), lambda r, *_: (r, 0, 0, 0))
    per_new = pl.BlockSpec((1, steps, features), lambda r, *_: (r, 0, 0))
    per_cache = pl.BlockSpec(memory_space=pl.ANY)
    out = pl.pallas_call(
        kernel,
        out_shape=jax.ShapeDtypeStruct((requests, steps, heads, head_dim), bf16),
        grid_spec=pltpu.PrefetchScalarGridSpec(
            num_scalar_prefetch=4,
            grid=(requests,),
            in_specs=[per_query, per_new, per_new, per_cache, per_cache],
            out_specs=per_query,
            scratch_shapes=[
                pltpu.VMEM((2, slots, features), key_cache.dtype),
                pltpu.VMEM((2, slots, features), value_cache.dtype),
                pltpu.SemaphoreType.DMA((2, 2, chunks)),
            ],
        ),
    )(
        lengths,
        merge_flags.reshape(-1),
        importance.reshape(-1),
        last_weight.reshape(-1),
        queries.reshape(requests, steps, heads, head_dim),
        keys_new,
        values_new,
        key_cache,
        value_cache,
    )
    return out.reshape(requests, steps, query_width)


def run_experts(arriving, expert_gate_up, expert_down):
    hidden_units = expert_down.shape[1]
    both = jnp.einsum(
        "sjcd,jdf->sjcf", arriving, expert_gate_up, preferred_element_type=jnp.float32
    )
    active = (jax.nn.silu(both[..., :hidden_units]) * both[..., hidden_units:]).astype(jnp.bfloat16)
    return jnp.einsum(
        "sjcf,jfd->sjcd", active, expert_down, preferred_element_type=jnp.float32
    ).astype(jnp.bfloat16)


def shards(
    queries,
    keys_new,
    values_new,
    importance,
    merge_flags,
    key_cache,
    value_cache,
    last_weight,
    lengths,
    residual,
    o_weight,
    norm_gain,
    expert_gate_up,
    expert_down,
    routes,
    route_weights,
):
    requests, steps, query_width = queries.shape
    attended = decode_attention(
        queries,
        keys_new,
        values_new,
        importance,
        merge_flags,
        key_cache,
        value_cache,
        last_weight,
        lengths,
    )
    rows = requests * steps
    width = o_weight.shape[1]
    gathered = lax.all_gather(o_weight, ("x", "c"), axis=0, tiled=True)
    lines = lax.axis_size("y")
    line = lax.axis_index("y")
    block = query_width // lines
    flat = attended.reshape(rows, query_width)

    def shifted(value, shift):
        return lax.ppermute(value, "y", [(j, (j + shift) % lines) for j in range(lines)])

    pieces = [lax.dynamic_slice_in_dim(flat, line * block, block, 1)]
    for shift in range(1, lines):
        piece = lax.dynamic_slice_in_dim(flat, ((line + shift) % lines) * block, block, 1)
        pieces.append(shifted(piece, shift))
    partials = jnp.dot(
        jnp.concatenate(pieces, axis=0), gathered, preferred_element_type=jnp.float32
    ).reshape(lines, rows, width)
    projected = partials[0]
    for shift in range(1, lines):
        sent = shifted(partials[shift].astype(jnp.bfloat16), lines - shift)
        projected = projected + sent.astype(jnp.float32)
    members = lax.axis_size("y") * lax.axis_size("x") * lax.axis_size("c")
    mixed = residual.reshape(rows, width).astype(jnp.float32) + projected
    normed = (
        mixed * lax.rsqrt(jnp.mean(mixed * mixed, axis=1, keepdims=True) + EPS) * norm_gain
    ).astype(jnp.bfloat16)
    experts_local = expert_gate_up.shape[0]
    dp_size = lax.axis_size("dp")
    experts_all = experts_local * dp_size * members
    top_k = routes.shape[2]
    capacity = max(2, 2 * rows * top_k // experts_all)
    chosen = routes.reshape(rows * top_k)
    sequence = jnp.arange(rows * top_k, dtype=jnp.int32)
    earlier = sequence[:, None] > sequence[None, :]
    rank = jnp.sum(((chosen[:, None] == chosen[None, :]) & earlier).astype(jnp.int32), axis=1)
    target = chosen * capacity + rank
    placing = (
        jnp.arange(experts_all * capacity, dtype=jnp.int32)[:, None] == target[None, :]
    ).reshape(experts_all, capacity, rows, top_k)
    placing = jnp.any(placing, axis=3).astype(jnp.bfloat16)
    outgoing = jnp.einsum(
        "ecr,rd->ecd", placing, normed, preferred_element_type=jnp.float32
    ).astype(jnp.bfloat16)
    arrived = lax.all_to_all(
        outgoing,
        ("dp", "y", "x", "c"),
        split_axis=0,
        concat_axis=0,
        tiled=True,
    )
    depth = arrived.shape[1]
    sources = arrived.shape[0] // experts_local
    answer = run_experts(
        arrived.reshape(sources, experts_local, depth, width), expert_gate_up, expert_down
    )
    returned = lax.all_to_all(
        answer.reshape(sources * experts_local, depth, width),
        ("dp", "y", "x", "c"),
        split_axis=0,
        concat_axis=0,
        tiled=True,
    )
    slots_all = jnp.arange(experts_all * capacity, dtype=jnp.int32)
    gathering = jnp.sum(
        jnp.where(
            slots_all[None, None, :] == target.reshape(rows, top_k, 1),
            route_weights.reshape(rows, top_k, 1),
            0.0,
        ),
        axis=1,
    ).reshape(rows, experts_all, capacity)
    blended = jnp.einsum(
        "tec,ecd->td",
        gathering,
        returned.astype(jnp.float32),
        precision=lax.Precision.HIGHEST,
        preferred_element_type=jnp.float32,
    )
    layer_out = (mixed + blended).astype(jnp.bfloat16).reshape(requests, steps, width)
    return (attended, layer_out)


def solution(mesh):
    lines = mesh.devices.shape[1] // 8
    mesh = jax.sharding.Mesh(
        mesh.devices.reshape(mesh.devices.shape[0], lines, 4, 2), ("dp", "y", "x", "c")
    )
    return jax.shard_map(
        shards,
        mesh=mesh,
        in_specs=(
            P(("dp", "y", "x", "c"), None, None),
            P(("dp", "y", "x", "c"), None, None),
            P(("dp", "y", "x", "c"), None, None),
            P(("dp", "y", "x", "c"), None, None),
            P(("dp", "y", "x", "c"), None, None),
            P(("dp", "y", "x", "c"), None, None),
            P(("dp", "y", "x", "c"), None, None),
            P(("dp", "y", "x", "c"), None),
            P(("dp", "y", "x", "c")),
            P(("dp", "y", "x", "c"), None, None),
            P(("y", "x", "c"), None),
            P(),
            P(("dp", "y", "x", "c"), None, None),
            P(("dp", "y", "x", "c"), None, None),
            P(("dp", "y", "x", "c"), None, None),
            P(("dp", "y", "x", "c"), None, None),
        ),
        out_specs=(P(("dp", "y", "x", "c"), None, None), P(("dp", "y", "x", "c"), None, None)),
        check_vma=False,
    )
```

```python
import functools
import math

import jax
import jax.numpy as jnp
from jax import lax
from jax.experimental import pallas as pl
from jax.experimental.pallas import tpu as pltpu
from jax.sharding import PartitionSpec as P

EPS = 1e-06


def decode_attention(queries, keys_new, values_new, importance, merge_flags, key_cache,
                     value_cache, last_weight, lengths):
    requests, steps, query_width = queries.shape
    heads_kv = last_weight.shape[1]
    slots, features = key_cache.shape[1], key_cache.shape[2]
    head_dim = features // heads_kv
    group = query_width // head_dim // heads_kv
    scale = 1.0 / math.sqrt(head_dim)
    f32, bf16 = jnp.float32, jnp.bfloat16

    chunk = math.gcd(slots, 128)
    window = 16

    chunks = slots // chunk

    def kernel(len_ref, flag_ref, share_ref, weight_ref, q_ref, kn_ref, vn_ref, k_hbm, v_hbm, o_ref,
               k_buf, v_buf, sems):
        r = pl.program_id(0)
        n = len_ref[r]
        here_buf = r % 2

        def copies(req, buf):
            needed = (len_ref[req] - 1) // chunk + 1
            for c in range(chunks):
                part = pl.ds(c * chunk, chunk)
                for a, (src, dst) in enumerate(((k_hbm, k_buf), (v_hbm, v_buf))):
                    copy = pltpu.make_async_copy(
                        src.at[req, part], dst.at[buf, part], sems.at[a, buf, c]
                    )
                    yield c < needed, copy

        def start_all(req, buf):
            for cond, copy in copies(req, buf):
                pl.when(cond)(copy.start)

        @pl.when(r == 0)
        def _():
            start_all(0, 0)

        @pl.when(r + 1 < requests)
        def _():
            start_all(r + 1, 1 - here_buf)

        for cond, copy in copies(r, here_buf):
            pl.when(cond)(copy.wait)
        k_ref = k_buf.at[here_buf]
        v_ref = v_buf.at[here_buf]
        start = pl.multiple_of(((n - 1) // window) * window, window)
        here = lax.broadcasted_iota(jnp.int32, (window, features), 0) == (n - 1 - start)
        last_k = jnp.sum(
            jnp.where(here, k_ref[pl.ds(start, window), :].astype(f32), 0.0), axis=0, keepdims=True
        )
        last_v = jnp.sum(
            jnp.where(here, v_ref[pl.ds(start, window), :].astype(f32), 0.0), axis=0, keepdims=True
        )
        new_k = kn_ref[0].astype(f32)
        new_v = vn_ref[0].astype(f32)

        def lane_mask(flag):
            return jnp.full((1, head_dim), flag, jnp.int32) == 1

        def row_mask(flag):
            return jnp.full((group, 1), flag, jnp.int32) == 1

        tails_of = []
        for g in range(heads_kv):
            lanes = slice(g * head_dim, (g + 1) * head_dim)
            z = weight_ref[r * heads_kv + g]
            f0 = flag_ref[(r * steps) * heads_kv + g]
            f1 = flag_ref[(r * steps + 1) * heads_kv + g]
            w0 = share_ref[(r * steps) * heads_kv + g]
            w1 = share_ref[(r * steps + 1) * heads_kv + g]
            z1 = jnp.where(f0 == 1, z + w0, w0)
            m0, m1 = lane_mask(f0), lane_mask(f1)
            both = lane_mask(f0 * f1)

            def settle(last, new):
                old0 = last[:, lanes]
                n0, n1 = new[0:1, lanes], new[1:2, lanes]
                b0 = ((z * old0 + w0 * n0) / (z + w0)).astype(bf16).astype(f32)
                a0 = jnp.where(m0, b0, old0)
                cur = jnp.where(m0, a0, n0)
                b1 = ((z1 * cur + w1 * n1) / (z1 + w1)).astype(bf16).astype(f32)
                second = (
                    jnp.where(both, b1, jnp.where(m0, a0, old0)),
                    jnp.where(m0, n1, jnp.where(m1, b1, n0)),
                    n1,
                )
                return (a0, n0), second

            count0 = 2 - f0
            tails_of.append((settle(last_k, new_k), settle(last_v, new_v), (count0, count0 + 1 - f1)))

        def attend(span):
            valid = lax.broadcasted_iota(jnp.int32, (steps * group, span), 1) < n - 1
            for g in range(heads_kv):
                lanes = slice(g * head_dim, (g + 1) * head_dim)
                keys_t, values_t, counts = tails_of[g]
                rows = slice(g * group, (g + 1) * group)
                q = jnp.concatenate([q_ref[0, t, rows, :] for t in range(steps)], axis=0)
                main = (
                    lax.dot_general(
                        q, k_ref[0:span, lanes], (((1,), (1,)), ((), ())),
                        preferred_element_type=f32,
                    )
                    * scale
                )
                main = jnp.where(valid, main, -jnp.inf)
                qf = q.astype(f32)
                top = jnp.max(main, axis=1, keepdims=True)
                tops, tails = [], []
                for t in range(steps):
                    here_rows = slice(t * group, (t + 1) * group)
                    top_t = top[here_rows]
                    step_tails = []
                    for j, (tk, tv) in enumerate(zip(keys_t[t], values_t[t])):
                        ts = jnp.sum(qf[here_rows] * tk, axis=1, keepdims=True) * scale
                        ts = jnp.where(row_mask((j < counts[t]).astype(jnp.int32)), ts, -jnp.inf)
                        top_t = jnp.maximum(top_t, ts)
                        step_tails.append((ts, tv))
                    tops.append(top_t)
                    tails.append(step_tails)
                top = jnp.concatenate(tops, axis=0)
                raw = jnp.exp(main - top)
                total = jnp.sum(raw, axis=1, keepdims=True)
                summed = jnp.dot(
                    raw.astype(bf16), v_ref[0:span, lanes], preferred_element_type=f32
                )
                for t in range(steps):
                    here_rows = slice(t * group, (t + 1) * group)
                    total_t = total[here_rows]
                    summed_t = summed[here_rows]
                    for ts, tv in tails[t]:
                        part = jnp.exp(ts - tops[t])
                        total_t = total_t + part
                        summed_t = summed_t + part.astype(bf16).astype(f32) * tv
                    o_ref[0, t, rows, :] = (summed_t / total_t).astype(bf16)

        used = (n - 1) // chunk + 1
        for k in range(1, slots // chunk + 1):
            pl.when(used == k)(functools.partial(attend, k * chunk))

    heads = query_width // head_dim
    per_query = pl.BlockSpec((1, steps, heads, head_dim), lambda r, *_: (r, 0, 0, 0))
    per_new = pl.BlockSpec((1, steps, features), lambda r, *_: (r, 0, 0))
    per_cache = pl.BlockSpec(memory_space=pl.ANY)
    out = pl.pallas_call(
        kernel,
        out_shape=jax.ShapeDtypeStruct((requests, steps, heads, head_dim), bf16),
        grid_spec=pltpu.PrefetchScalarGridSpec(
            num_scalar_prefetch=4,
            grid=(requests,),
            in_specs=[per_query, per_new, per_new, per_cache, per_cache],
            out_specs=per_query,
            scratch_shapes=[
                pltpu.VMEM((2, slots, features), key_cache.dtype),
                pltpu.VMEM((2, slots, features), value_cache.dtype),
                pltpu.SemaphoreType.DMA((2, 2, chunks)),
            ],
        ),
    )(
        lengths,
        merge_flags.reshape(-1),
        importance.reshape(-1),
        last_weight.reshape(-1),
        queries.reshape(requests, steps, heads, head_dim),
        keys_new,
        values_new,
        key_cache,
        value_cache,
    )
    return out.reshape(requests, steps, query_width)


def run_experts(arriving, expert_gate_up, expert_down):
    hidden_units = expert_down.shape[1]
    both = jnp.einsum(
        "sjcd,jdf->sjcf", arriving, expert_gate_up, preferred_element_type=jnp.float32
    )
    active = (jax.nn.silu(both[..., :hidden_units]) * both[..., hidden_units:]).astype(jnp.bfloat16)
    return jnp.einsum(
        "sjcf,jfd->sjcd", active, expert_down, preferred_element_type=jnp.float32
    ).astype(jnp.bfloat16)


def shards(
    queries,
    keys_new,
    values_new,
    importance,
    merge_flags,
    key_cache,
    value_cache,
    last_weight,
    lengths,
    residual,
    o_weight,
    norm_gain,
    expert_gate_up,
    expert_down,
    routes,
    route_weights,
):
    requests, steps, query_width = queries.shape
    attended = decode_attention(
        queries,
        keys_new,
        values_new,
        importance,
        merge_flags,
        key_cache,
        value_cache,
        last_weight,
        lengths,
    )
    rows = requests * steps
    width = o_weight.shape[1]
    cols, cores = lax.axis_size("x"), lax.axis_size("c")
    col, core = lax.axis_index("x"), lax.axis_index("c")
    part = o_weight.shape[0]

    def along(value, axis, size, shift):
        return lax.ppermute(value, axis, [(j, (j + shift) % size) for j in range(size)])

    near = jnp.concatenate(
        [o_weight] + [along(o_weight, "x", cols, shift) for shift in range(1, cols)], axis=0
    )
    near, ready = lax.optimization_barrier((near, attended))
    far = along(near, "c", cores, 1)
    lines = lax.axis_size("y")
    line = lax.axis_index("y")
    block = query_width // lines
    flat = ready.reshape(rows, query_width)

    def shifted(value, shift):
        return lax.ppermute(value, "y", [(j, (j + shift) % lines) for j in range(lines)])

    pieces = [lax.dynamic_slice_in_dim(flat, line * block, block, 1)]
    for shift in range(1, lines):
        piece = lax.dynamic_slice_in_dim(flat, ((line + shift) % lines) * block, block, 1)
        pieces.append(shifted(piece, shift))
    stacked = jnp.concatenate(pieces, axis=0)

    def columns(owner):
        return jnp.concatenate(
            [
                lax.dynamic_slice_in_dim(
                    stacked, (((col - j) % cols) * cores + owner) * part, part, 1
                )
                for j in range(cols)
            ],
            axis=1,
        )

    partials = (
        jnp.dot(columns(core), near, preferred_element_type=jnp.float32)
        + jnp.dot(columns((core + cores - 1) % cores), far, preferred_element_type=jnp.float32)
    ).reshape(lines, rows, width)
    projected = partials[0]
    for shift in range(1, lines):
        sent = shifted(partials[shift].astype(jnp.bfloat16), lines - shift)
        projected = projected + sent.astype(jnp.float32)
    members = lax.axis_size("y") * lax.axis_size("x") * lax.axis_size("c")
    mixed = residual.reshape(rows, width).astype(jnp.float32) + projected
    normed = (
        mixed * lax.rsqrt(jnp.mean(mixed * mixed, axis=1, keepdims=True) + EPS) * norm_gain
    ).astype(jnp.bfloat16)
    experts_local = expert_gate_up.shape[0]
    dp_size = lax.axis_size("dp")
    experts_all = experts_local * dp_size * members
    top_k = routes.shape[2]
    capacity = max(2, 2 * rows * top_k // experts_all)
    chosen = routes.reshape(rows * top_k)
    sequence = jnp.arange(rows * top_k, dtype=jnp.int32)
    earlier = sequence[:, None] > sequence[None, :]
    rank = jnp.sum(((chosen[:, None] == chosen[None, :]) & earlier).astype(jnp.int32), axis=1)
    target = chosen * capacity + rank
    placing = (
        jnp.arange(experts_all * capacity, dtype=jnp.int32)[:, None] == target[None, :]
    ).reshape(experts_all, capacity, rows, top_k)
    placing = jnp.any(placing, axis=3).astype(jnp.bfloat16)
    outgoing = jnp.einsum(
        "ecr,rd->ecd", placing, normed, preferred_element_type=jnp.float32
    ).astype(jnp.bfloat16)
    arrived = lax.all_to_all(
        outgoing,
        ("dp", "y", "x", "c"),
        split_axis=0,
        concat_axis=0,
        tiled=True,
    )
    depth = arrived.shape[1]
    sources = arrived.shape[0] // experts_local
    answer = run_experts(
        arrived.reshape(sources, experts_local, depth, width), expert_gate_up, expert_down
    )
    returned = lax.all_to_all(
        answer.reshape(sources * experts_local, depth, width),
        ("dp", "y", "x", "c"),
        split_axis=0,
        concat_axis=0,
        tiled=True,
    )
    slots_all = jnp.arange(experts_all * capacity, dtype=jnp.int32)
    gathering = jnp.sum(
        jnp.where(
            slots_all[None, None, :] == target.reshape(rows, top_k, 1),
            route_weights.reshape(rows, top_k, 1),
            0.0,
        ),
        axis=1,
    ).reshape(rows, experts_all, capacity)
    blended = jnp.einsum(
        "tec,ecd->td",
        gathering,
        returned.astype(jnp.float32),
        precision=lax.Precision.HIGHEST,
        preferred_element_type=jnp.float32,
    )
    layer_out = (mixed + blended).astype(jnp.bfloat16).reshape(requests, steps, width)
    return (attended, layer_out)


def solution(mesh):
    lines = mesh.devices.shape[1] // 8
    mesh = jax.sharding.Mesh(
        mesh.devices.reshape(mesh.devices.shape[0], lines, 4, 2), ("dp", "y", "x", "c")
    )
    return jax.shard_map(
        shards,
        mesh=mesh,
        in_specs=(
            P(("dp", "y", "x", "c"), None, None),
            P(("dp", "y", "x", "c"), None, None),
            P(("dp", "y", "x", "c"), None, None),
            P(("dp", "y", "x", "c"), None, None),
            P(("dp", "y", "x", "c"), None, None),
            P(("dp", "y", "x", "c"), None, None),
            P(("dp", "y", "x", "c"), None, None),
            P(("dp", "y", "x", "c"), None),
            P(("dp", "y", "x", "c")),
            P(("dp", "y", "x", "c"), None, None),
            P(("y", "x", "c"), None),
            P(),
            P(("dp", "y", "x", "c"), None, None),
            P(("dp", "y", "x", "c"), None, None),
            P(("dp", "y", "x", "c"), None, None),
            P(("dp", "y", "x", "c"), None, None),
        ),
        out_specs=(P(("dp", "y", "x", "c"), None, None), P(("dp", "y", "x", "c"), None, None)),
        check_vma=False,
    )
```

```python
import functools
import math

import jax
import jax.numpy as jnp
from jax import lax
from jax.experimental import pallas as pl
from jax.experimental.pallas import tpu as pltpu
from jax.sharding import PartitionSpec as P

EPS = 1e-06


def decode_attention(queries, keys_new, values_new, importance, merge_flags, key_cache,
                     value_cache, last_weight, lengths):
    requests, steps, query_width = queries.shape
    heads_kv = last_weight.shape[1]
    slots, features = key_cache.shape[1], key_cache.shape[2]
    head_dim = features // heads_kv
    group = query_width // head_dim // heads_kv
    scale = 1.0 / math.sqrt(head_dim)
    f32, bf16 = jnp.float32, jnp.bfloat16

    chunk = math.gcd(slots, 128)
    window = 16

    chunks = slots // chunk

    def kernel(len_ref, flag_ref, share_ref, weight_ref, q_ref, kn_ref, vn_ref, k_hbm, v_hbm, o_ref,
               k_buf, v_buf, sems):
        r = pl.program_id(0)
        n = len_ref[r]
        here_buf = r % 2

        def copies(req, buf):
            needed = (len_ref[req] - 1) // chunk + 1
            for c in range(chunks):
                part = pl.ds(c * chunk, chunk)
                for a, (src, dst) in enumerate(((k_hbm, k_buf), (v_hbm, v_buf))):
                    copy = pltpu.make_async_copy(
                        src.at[req, part], dst.at[buf, part], sems.at[a, buf, c]
                    )
                    yield c < needed, copy

        def start_all(req, buf):
            for cond, copy in copies(req, buf):
                pl.when(cond)(copy.start)

        @pl.when(r == 0)
        def _():
            start_all(0, 0)

        @pl.when(r + 1 < requests)
        def _():
            start_all(r + 1, 1 - here_buf)

        for cond, copy in copies(r, here_buf):
            pl.when(cond)(copy.wait)
        k_ref = k_buf.at[here_buf]
        v_ref = v_buf.at[here_buf]
        start = pl.multiple_of(((n - 1) // window) * window, window)
        here = lax.broadcasted_iota(jnp.int32, (window, features), 0) == (n - 1 - start)
        last_k = jnp.sum(
            jnp.where(here, k_ref[pl.ds(start, window), :].astype(f32), 0.0), axis=0, keepdims=True
        )
        last_v = jnp.sum(
            jnp.where(here, v_ref[pl.ds(start, window), :].astype(f32), 0.0), axis=0, keepdims=True
        )
        new_k = kn_ref[0].astype(f32)
        new_v = vn_ref[0].astype(f32)

        def lane_mask(flag):
            return jnp.full((1, head_dim), flag, jnp.int32) == 1

        def row_mask(flag):
            return jnp.full((group, 1), flag, jnp.int32) == 1

        tails_of = []
        for g in range(heads_kv):
            lanes = slice(g * head_dim, (g + 1) * head_dim)
            z = weight_ref[r * heads_kv + g]
            f0 = flag_ref[(r * steps) * heads_kv + g]
            f1 = flag_ref[(r * steps + 1) * heads_kv + g]
            w0 = share_ref[(r * steps) * heads_kv + g]
            w1 = share_ref[(r * steps + 1) * heads_kv + g]
            z1 = jnp.where(f0 == 1, z + w0, w0)
            m0, m1 = lane_mask(f0), lane_mask(f1)
            both = lane_mask(f0 * f1)

            def settle(last, new):
                old0 = last[:, lanes]
                n0, n1 = new[0:1, lanes], new[1:2, lanes]
                b0 = ((z * old0 + w0 * n0) / (z + w0)).astype(bf16).astype(f32)
                a0 = jnp.where(m0, b0, old0)
                cur = jnp.where(m0, a0, n0)
                b1 = ((z1 * cur + w1 * n1) / (z1 + w1)).astype(bf16).astype(f32)
                second = (
                    jnp.where(both, b1, jnp.where(m0, a0, old0)),
                    jnp.where(m0, n1, jnp.where(m1, b1, n0)),
                    n1,
                )
                return (a0, n0), second

            count0 = 2 - f0
            tails_of.append((settle(last_k, new_k), settle(last_v, new_v), (count0, count0 + 1 - f1)))

        def attend(span):
            valid = lax.broadcasted_iota(jnp.int32, (steps * group, span), 1) < n - 1
            for g in range(heads_kv):
                lanes = slice(g * head_dim, (g + 1) * head_dim)
                keys_t, values_t, counts = tails_of[g]
                rows = slice(g * group, (g + 1) * group)
                q = jnp.concatenate([q_ref[0, t, rows, :] for t in range(steps)], axis=0)
                main = (
                    lax.dot_general(
                        q, k_ref[0:span, lanes], (((1,), (1,)), ((), ())),
                        preferred_element_type=f32,
                    )
                    * scale
                )
                main = jnp.where(valid, main, -jnp.inf)
                qf = q.astype(f32)
                top = jnp.max(main, axis=1, keepdims=True)
                tops, tails = [], []
                for t in range(steps):
                    here_rows = slice(t * group, (t + 1) * group)
                    top_t = top[here_rows]
                    step_tails = []
                    for j, (tk, tv) in enumerate(zip(keys_t[t], values_t[t])):
                        ts = jnp.sum(qf[here_rows] * tk, axis=1, keepdims=True) * scale
                        ts = jnp.where(row_mask((j < counts[t]).astype(jnp.int32)), ts, -jnp.inf)
                        top_t = jnp.maximum(top_t, ts)
                        step_tails.append((ts, tv))
                    tops.append(top_t)
                    tails.append(step_tails)
                top = jnp.concatenate(tops, axis=0)
                raw = jnp.exp(main - top)
                total = jnp.sum(raw, axis=1, keepdims=True)
                summed = jnp.dot(
                    raw.astype(bf16), v_ref[0:span, lanes], preferred_element_type=f32
                )
                for t in range(steps):
                    here_rows = slice(t * group, (t + 1) * group)
                    total_t = total[here_rows]
                    summed_t = summed[here_rows]
                    for ts, tv in tails[t]:
                        part = jnp.exp(ts - tops[t])
                        total_t = total_t + part
                        summed_t = summed_t + part.astype(bf16).astype(f32) * tv
                    o_ref[0, t, rows, :] = (summed_t / total_t).astype(bf16)

        used = (n - 1) // chunk + 1
        for k in range(1, slots // chunk + 1):
            pl.when(used == k)(functools.partial(attend, k * chunk))

    heads = query_width // head_dim
    per_query = pl.BlockSpec((1, steps, heads, head_dim), lambda r, *_: (r, 0, 0, 0))
    per_new = pl.BlockSpec((1, steps, features), lambda r, *_: (r, 0, 0))
    per_cache = pl.BlockSpec(memory_space=pl.ANY)
    out = pl.pallas_call(
        kernel,
        out_shape=jax.ShapeDtypeStruct((requests, steps, heads, head_dim), bf16),
        grid_spec=pltpu.PrefetchScalarGridSpec(
            num_scalar_prefetch=4,
            grid=(requests,),
            in_specs=[per_query, per_new, per_new, per_cache, per_cache],
            out_specs=per_query,
            scratch_shapes=[
                pltpu.VMEM((2, slots, features), key_cache.dtype),
                pltpu.VMEM((2, slots, features), value_cache.dtype),
                pltpu.SemaphoreType.DMA((2, 2, chunks)),
            ],
        ),
    )(
        lengths,
        merge_flags.reshape(-1),
        importance.reshape(-1),
        last_weight.reshape(-1),
        queries.reshape(requests, steps, heads, head_dim),
        keys_new,
        values_new,
        key_cache,
        value_cache,
    )
    return out.reshape(requests, steps, query_width)


def run_experts(arriving, expert_gate_up, expert_down):
    hidden_units = expert_down.shape[1]
    both = jnp.einsum(
        "sjcd,jdf->sjcf", arriving, expert_gate_up, preferred_element_type=jnp.float32
    )
    active = (jax.nn.silu(both[..., :hidden_units]) * both[..., hidden_units:]).astype(jnp.bfloat16)
    return jnp.einsum(
        "sjcf,jfd->sjcd", active, expert_down, preferred_element_type=jnp.float32
    ).astype(jnp.bfloat16)


def shards(
    queries,
    keys_new,
    values_new,
    importance,
    merge_flags,
    key_cache,
    value_cache,
    last_weight,
    lengths,
    residual,
    o_weight,
    norm_gain,
    expert_gate_up,
    expert_down,
    routes,
    route_weights,
):
    requests, steps, query_width = queries.shape
    attended = decode_attention(
        queries,
        keys_new,
        values_new,
        importance,
        merge_flags,
        key_cache,
        value_cache,
        last_weight,
        lengths,
    )
    rows = requests * steps
    width = o_weight.shape[1]
    cols, cores = lax.axis_size("x"), lax.axis_size("c")
    col, core = lax.axis_index("x"), lax.axis_index("c")
    part = o_weight.shape[0]

    def along(value, axis, size, shift):
        return lax.ppermute(value, axis, [(j, (j + shift) % size) for j in range(size)])

    fetched = [along(o_weight, "x", cols, shift) for shift in range(1, cols)]
    lines = lax.axis_size("y")
    line = lax.axis_index("y")
    block = query_width // lines
    flat = attended.reshape(rows, query_width)

    def shifted(value, shift):
        return lax.ppermute(value, "y", [(j, (j + shift) % lines) for j in range(lines)])

    pieces = [lax.dynamic_slice_in_dim(flat, line * block, block, 1)]
    for shift in range(1, lines):
        piece = lax.dynamic_slice_in_dim(flat, ((line + shift) % lines) * block, block, 1)
        pieces.append(shifted(piece, shift))
    fetched, pieces = lax.optimization_barrier((fetched, pieces))
    near = jnp.concatenate([o_weight] + fetched, axis=0)
    far = along(near, "c", cores, 1)
    stacked = jnp.concatenate(pieces, axis=0)

    def columns(owner):
        return jnp.concatenate(
            [
                lax.dynamic_slice_in_dim(
                    stacked, (((col - j) % cols) * cores + owner) * part, part, 1
                )
                for j in range(cols)
            ],
            axis=1,
        )

    partials = (
        jnp.dot(columns(core), near, preferred_element_type=jnp.float32)
        + jnp.dot(columns((core + cores - 1) % cores), far, preferred_element_type=jnp.float32)
    ).reshape(lines, rows, width)
    projected = partials[0]
    for shift in range(1, lines):
        sent = shifted(partials[shift].astype(jnp.bfloat16), lines - shift)
        projected = projected + sent.astype(jnp.float32)
    members = lax.axis_size("y") * lax.axis_size("x") * lax.axis_size("c")
    mixed = residual.reshape(rows, width).astype(jnp.float32) + projected
    normed = (
        mixed * lax.rsqrt(jnp.mean(mixed * mixed, axis=1, keepdims=True) + EPS) * norm_gain
    ).astype(jnp.bfloat16)
    experts_local = expert_gate_up.shape[0]
    dp_size = lax.axis_size("dp")
    experts_all = experts_local * dp_size * members
    top_k = routes.shape[2]
    capacity = max(2, 2 * rows * top_k // experts_all)
    chosen = routes.reshape(rows * top_k)
    sequence = jnp.arange(rows * top_k, dtype=jnp.int32)
    earlier = sequence[:, None] > sequence[None, :]
    rank = jnp.sum(((chosen[:, None] == chosen[None, :]) & earlier).astype(jnp.int32), axis=1)
    target = chosen * capacity + rank
    placing = (
        jnp.arange(experts_all * capacity, dtype=jnp.int32)[:, None] == target[None, :]
    ).reshape(experts_all, capacity, rows, top_k)
    placing = jnp.any(placing, axis=3).astype(jnp.bfloat16)
    outgoing = jnp.einsum(
        "ecr,rd->ecd", placing, normed, preferred_element_type=jnp.float32
    ).astype(jnp.bfloat16)
    arrived = lax.all_to_all(
        outgoing,
        ("dp", "y", "x", "c"),
        split_axis=0,
        concat_axis=0,
        tiled=True,
    )
    depth = arrived.shape[1]
    sources = arrived.shape[0] // experts_local
    answer = run_experts(
        arrived.reshape(sources, experts_local, depth, width), expert_gate_up, expert_down
    )
    returned = lax.all_to_all(
        answer.reshape(sources * experts_local, depth, width),
        ("dp", "y", "x", "c"),
        split_axis=0,
        concat_axis=0,
        tiled=True,
    )
    slots_all = jnp.arange(experts_all * capacity, dtype=jnp.int32)
    gathering = jnp.sum(
        jnp.where(
            slots_all[None, None, :] == target.reshape(rows, top_k, 1),
            route_weights.reshape(rows, top_k, 1),
            0.0,
        ),
        axis=1,
    ).reshape(rows, experts_all, capacity)
    blended = jnp.einsum(
        "tec,ecd->td",
        gathering,
        returned.astype(jnp.float32),
        precision=lax.Precision.HIGHEST,
        preferred_element_type=jnp.float32,
    )
    layer_out = (mixed + blended).astype(jnp.bfloat16).reshape(requests, steps, width)
    return (attended, layer_out)


def solution(mesh):
    lines = mesh.devices.shape[1] // 8
    mesh = jax.sharding.Mesh(
        mesh.devices.reshape(mesh.devices.shape[0], lines, 4, 2), ("dp", "y", "x", "c")
    )
    return jax.shard_map(
        shards,
        mesh=mesh,
        in_specs=(
            P(("dp", "y", "x", "c"), None, None),
            P(("dp", "y", "x", "c"), None, None),
            P(("dp", "y", "x", "c"), None, None),
            P(("dp", "y", "x", "c"), None, None),
            P(("dp", "y", "x", "c"), None, None),
            P(("dp", "y", "x", "c"), None, None),
            P(("dp", "y", "x", "c"), None, None),
            P(("dp", "y", "x", "c"), None),
            P(("dp", "y", "x", "c")),
            P(("dp", "y", "x", "c"), None, None),
            P(("y", "x", "c"), None),
            P(),
            P(("dp", "y", "x", "c"), None, None),
            P(("dp", "y", "x", "c"), None, None),
            P(("dp", "y", "x", "c"), None, None),
            P(("dp", "y", "x", "c"), None, None),
        ),
        out_specs=(P(("dp", "y", "x", "c"), None, None), P(("dp", "y", "x", "c"), None, None)),
        check_vma=False,
    )
```

```python
import functools
import math

import jax
import jax.numpy as jnp
from jax import lax
from jax.experimental import pallas as pl
from jax.experimental.pallas import tpu as pltpu
from jax.sharding import PartitionSpec as P

EPS = 1e-06


def decode_attention(queries, keys_new, values_new, importance, merge_flags, key_cache,
                     value_cache, last_weight, lengths):
    requests, steps, query_width = queries.shape
    heads_kv = last_weight.shape[1]
    slots, features = key_cache.shape[1], key_cache.shape[2]
    head_dim = features // heads_kv
    group = query_width // head_dim // heads_kv
    scale = 1.0 / math.sqrt(head_dim)
    f32, bf16 = jnp.float32, jnp.bfloat16

    chunk = math.gcd(slots, 128)
    window = 16

    chunks = slots // chunk

    def kernel(len_ref, flag_ref, share_ref, weight_ref, q_ref, kn_ref, vn_ref, k_hbm, v_hbm, o_ref,
               k_buf, v_buf, sems):
        r = pl.program_id(0)
        n = len_ref[r]
        here_buf = r % 2

        def copies(req, buf):
            needed = (len_ref[req] - 1) // chunk + 1
            for c in range(chunks):
                part = pl.ds(c * chunk, chunk)
                for a, (src, dst) in enumerate(((k_hbm, k_buf), (v_hbm, v_buf))):
                    copy = pltpu.make_async_copy(
                        src.at[req, part], dst.at[buf, part], sems.at[a, buf, c]
                    )
                    yield c < needed, copy

        def start_all(req, buf):
            for cond, copy in copies(req, buf):
                pl.when(cond)(copy.start)

        @pl.when(r == 0)
        def _():
            start_all(0, 0)

        @pl.when(r + 1 < requests)
        def _():
            start_all(r + 1, 1 - here_buf)

        for cond, copy in copies(r, here_buf):
            pl.when(cond)(copy.wait)
        k_ref = k_buf.at[here_buf]
        v_ref = v_buf.at[here_buf]
        start = pl.multiple_of(((n - 1) // window) * window, window)
        here = lax.broadcasted_iota(jnp.int32, (window, features), 0) == (n - 1 - start)
        last_k = jnp.sum(
            jnp.where(here, k_ref[pl.ds(start, window), :].astype(f32), 0.0), axis=0, keepdims=True
        )
        last_v = jnp.sum(
            jnp.where(here, v_ref[pl.ds(start, window), :].astype(f32), 0.0), axis=0, keepdims=True
        )
        new_k = kn_ref[0].astype(f32)
        new_v = vn_ref[0].astype(f32)

        def lane_mask(flag):
            return jnp.full((1, head_dim), flag, jnp.int32) == 1

        def row_mask(flag):
            return jnp.full((group, 1), flag, jnp.int32) == 1

        tails_of = []
        for g in range(heads_kv):
            lanes = slice(g * head_dim, (g + 1) * head_dim)
            z = weight_ref[r * heads_kv + g]
            f0 = flag_ref[(r * steps) * heads_kv + g]
            f1 = flag_ref[(r * steps + 1) * heads_kv + g]
            w0 = share_ref[(r * steps) * heads_kv + g]
            w1 = share_ref[(r * steps + 1) * heads_kv + g]
            z1 = jnp.where(f0 == 1, z + w0, w0)
            m0, m1 = lane_mask(f0), lane_mask(f1)
            both = lane_mask(f0 * f1)

            def settle(last, new):
                old0 = last[:, lanes]
                n0, n1 = new[0:1, lanes], new[1:2, lanes]
                b0 = ((z * old0 + w0 * n0) / (z + w0)).astype(bf16).astype(f32)
                a0 = jnp.where(m0, b0, old0)
                cur = jnp.where(m0, a0, n0)
                b1 = ((z1 * cur + w1 * n1) / (z1 + w1)).astype(bf16).astype(f32)
                second = (
                    jnp.where(both, b1, jnp.where(m0, a0, old0)),
                    jnp.where(m0, n1, jnp.where(m1, b1, n0)),
                    n1,
                )
                return (a0, n0), second

            count0 = 2 - f0
            tails_of.append((settle(last_k, new_k), settle(last_v, new_v), (count0, count0 + 1 - f1)))

        def attend(span):
            valid = lax.broadcasted_iota(jnp.int32, (steps * group, span), 1) < n - 1
            for g in range(heads_kv):
                lanes = slice(g * head_dim, (g + 1) * head_dim)
                keys_t, values_t, counts = tails_of[g]
                rows = slice(g * group, (g + 1) * group)
                q = jnp.concatenate([q_ref[0, t, rows, :] for t in range(steps)], axis=0)
                main = (
                    lax.dot_general(
                        q, k_ref[0:span, lanes], (((1,), (1,)), ((), ())),
                        preferred_element_type=f32,
                    )
                    * scale
                )
                main = jnp.where(valid, main, -jnp.inf)
                qf = q.astype(f32)
                top = jnp.max(main, axis=1, keepdims=True)
                tops, tails = [], []
                for t in range(steps):
                    here_rows = slice(t * group, (t + 1) * group)
                    top_t = top[here_rows]
                    step_tails = []
                    for j, (tk, tv) in enumerate(zip(keys_t[t], values_t[t])):
                        ts = jnp.sum(qf[here_rows] * tk, axis=1, keepdims=True) * scale
                        ts = jnp.where(row_mask((j < counts[t]).astype(jnp.int32)), ts, -jnp.inf)
                        top_t = jnp.maximum(top_t, ts)
                        step_tails.append((ts, tv))
                    tops.append(top_t)
                    tails.append(step_tails)
                top = jnp.concatenate(tops, axis=0)
                raw = jnp.exp(main - top)
                total = jnp.sum(raw, axis=1, keepdims=True)
                summed = jnp.dot(
                    raw.astype(bf16), v_ref[0:span, lanes], preferred_element_type=f32
                )
                for t in range(steps):
                    here_rows = slice(t * group, (t + 1) * group)
                    total_t = total[here_rows]
                    summed_t = summed[here_rows]
                    for ts, tv in tails[t]:
                        part = jnp.exp(ts - tops[t])
                        total_t = total_t + part
                        summed_t = summed_t + part.astype(bf16).astype(f32) * tv
                    o_ref[0, t, rows, :] = (summed_t / total_t).astype(bf16)

        used = (n - 1) // chunk + 1
        for k in range(1, slots // chunk + 1):
            pl.when(used == k)(functools.partial(attend, k * chunk))

    heads = query_width // head_dim
    per_query = pl.BlockSpec((1, steps, heads, head_dim), lambda r, *_: (r, 0, 0, 0))
    per_new = pl.BlockSpec((1, steps, features), lambda r, *_: (r, 0, 0))
    per_cache = pl.BlockSpec(memory_space=pl.ANY)
    out = pl.pallas_call(
        kernel,
        out_shape=jax.ShapeDtypeStruct((requests, steps, heads, head_dim), bf16),
        grid_spec=pltpu.PrefetchScalarGridSpec(
            num_scalar_prefetch=4,
            grid=(requests,),
            in_specs=[per_query, per_new, per_new, per_cache, per_cache],
            out_specs=per_query,
            scratch_shapes=[
                pltpu.VMEM((2, slots, features), key_cache.dtype),
                pltpu.VMEM((2, slots, features), value_cache.dtype),
                pltpu.SemaphoreType.DMA((2, 2, chunks)),
            ],
        ),
    )(
        lengths,
        merge_flags.reshape(-1),
        importance.reshape(-1),
        last_weight.reshape(-1),
        queries.reshape(requests, steps, heads, head_dim),
        keys_new,
        values_new,
        key_cache,
        value_cache,
    )
    return out.reshape(requests, steps, query_width)


def run_experts(arriving, expert_gate_up, expert_down):
    hidden_units = expert_down.shape[1]
    both = jnp.einsum(
        "sjcd,jdf->sjcf", arriving, expert_gate_up, preferred_element_type=jnp.float32
    )
    active = (jax.nn.silu(both[..., :hidden_units]) * both[..., hidden_units:]).astype(jnp.bfloat16)
    return jnp.einsum(
        "sjcf,jfd->sjcd", active, expert_down, preferred_element_type=jnp.float32
    ).astype(jnp.bfloat16)


def shards(
    queries,
    keys_new,
    values_new,
    importance,
    merge_flags,
    key_cache,
    value_cache,
    last_weight,
    lengths,
    residual,
    o_weight,
    norm_gain,
    expert_gate_up,
    expert_down,
    routes,
    route_weights,
):
    requests, steps, query_width = queries.shape
    attended = decode_attention(
        queries,
        keys_new,
        values_new,
        importance,
        merge_flags,
        key_cache,
        value_cache,
        last_weight,
        lengths,
    )
    rows = requests * steps
    width = o_weight.shape[1]
    gathered = lax.all_gather(o_weight, ("x", "c"), axis=0, tiled=True)
    lines = lax.axis_size("y")
    line = lax.axis_index("y")
    block = query_width // lines
    flat = attended.reshape(rows, query_width)

    def shifted(value, shift):
        return lax.ppermute(value, "y", [(j, (j + shift) % lines) for j in range(lines)])

    pieces = [lax.dynamic_slice_in_dim(flat, line * block, block, 1)]
    for shift in range(1, lines):
        piece = lax.dynamic_slice_in_dim(flat, ((line + shift) % lines) * block, block, 1)
        pieces.append(shifted(piece, shift))
    partials = jnp.dot(
        jnp.concatenate(pieces, axis=0), gathered, preferred_element_type=jnp.float32
    ).reshape(lines, rows, width)
    projected = partials[0]
    for shift in range(1, lines):
        sent = shifted(partials[shift].astype(jnp.bfloat16), lines - shift)
        projected = projected + sent.astype(jnp.float32)
    members = lax.axis_size("y") * lax.axis_size("x") * lax.axis_size("c")
    mixed = residual.reshape(rows, width).astype(jnp.float32) + projected
    normed = (
        mixed * lax.rsqrt(jnp.mean(mixed * mixed, axis=1, keepdims=True) + EPS) * norm_gain
    ).astype(jnp.bfloat16)
    experts_local = expert_gate_up.shape[0]
    dp_size = lax.axis_size("dp")
    experts_all = experts_local * dp_size * members
    top_k = routes.shape[2]
    capacity = max(2, 2 * rows * top_k // experts_all)
    chosen = routes.reshape(rows * top_k)
    sequence = jnp.arange(rows * top_k, dtype=jnp.int32)
    earlier = sequence[:, None] > sequence[None, :]
    rank = jnp.sum(((chosen[:, None] == chosen[None, :]) & earlier).astype(jnp.int32), axis=1)
    target = chosen * capacity + rank
    placing = (
        jnp.arange(experts_all * capacity, dtype=jnp.int32)[:, None] == target[None, :]
    ).reshape(experts_all, capacity, rows, top_k)
    placing = jnp.any(placing, axis=3).astype(jnp.bfloat16)
    outgoing = jnp.einsum(
        "ecr,rd->ecd", placing, normed, preferred_element_type=jnp.float32
    ).astype(jnp.bfloat16)
    arrived = lax.all_to_all(
        outgoing,
        ("dp", "y", "x", "c"),
        split_axis=0,
        concat_axis=0,
        tiled=True,
    )
    depth = arrived.shape[1]
    sources = arrived.shape[0] // experts_local
    answer = run_experts(
        arrived.reshape(sources, experts_local, depth, width), expert_gate_up, expert_down
    )
    returned = lax.all_to_all(
        answer.reshape(sources * experts_local, depth, width),
        ("dp", "y", "x", "c"),
        split_axis=0,
        concat_axis=0,
        tiled=True,
    )
    slots_all = jnp.arange(experts_all * capacity, dtype=jnp.int32)
    gathering = jnp.sum(
        jnp.where(
            slots_all[None, None, :] == target.reshape(rows, top_k, 1),
            route_weights.reshape(rows, top_k, 1),
            0.0,
        ),
        axis=1,
    ).reshape(rows, experts_all, capacity)
    high = gathering.astype(jnp.bfloat16)
    low = (gathering - high.astype(jnp.float32)).astype(jnp.bfloat16)
    blended = jnp.einsum(
        "tec,ecd->td", high, returned, preferred_element_type=jnp.float32
    ) + jnp.einsum("tec,ecd->td", low, returned, preferred_element_type=jnp.float32)
    layer_out = (mixed + blended).astype(jnp.bfloat16).reshape(requests, steps, width)
    return (attended, layer_out)


def solution(mesh):
    lines = mesh.devices.shape[1] // 8
    mesh = jax.sharding.Mesh(
        mesh.devices.reshape(mesh.devices.shape[0], lines, 4, 2), ("dp", "y", "x", "c")
    )
    return jax.shard_map(
        shards,
        mesh=mesh,
        in_specs=(
            P(("dp", "y", "x", "c"), None, None),
            P(("dp", "y", "x", "c"), None, None),
            P(("dp", "y", "x", "c"), None, None),
            P(("dp", "y", "x", "c"), None, None),
            P(("dp", "y", "x", "c"), None, None),
            P(("dp", "y", "x", "c"), None, None),
            P(("dp", "y", "x", "c"), None, None),
            P(("dp", "y", "x", "c"), None),
            P(("dp", "y", "x", "c")),
            P(("dp", "y", "x", "c"), None, None),
            P(("y", "x", "c"), None),
            P(),
            P(("dp", "y", "x", "c"), None, None),
            P(("dp", "y", "x", "c"), None, None),
            P(("dp", "y", "x", "c"), None, None),
            P(("dp", "y", "x", "c"), None, None),
        ),
        out_specs=(P(("dp", "y", "x", "c"), None, None), P(("dp", "y", "x", "c"), None, None)),
        check_vma=False,
    )
```
